256 devices in a mesh: tm: 32 (over x_lo, z, core), quad: 8 (over y, x_hi).
Axes of the slice: x: 4 (x_hi: 2, x_lo: 2; x = x_hi * 2 + x_lo), y: 4, z: 8, core: 2. Of those that a mesh axis runs over, the one named last changes fastest.
Arguments:
- features: bfloat16 [32, 2048, 192], P('tm', 'quad'), may hold values from -14 to 14
- w_query: bfloat16 [192, 192], replicated, may hold values from -1.25 to 1.25
- w_key: bfloat16 [192, 192], replicated, may hold values from -0.4375 to 0.4375
- w_value: bfloat16 [192, 192], replicated, may hold values from -0.4375 to 0.4375
- w_out: bfloat16 [192, 192], replicated, may hold values from -1.75 to 1.75
- block_offset: int32 [32, 16, 24], P('tm', 'quad'), may hold values from 0 to 2
- block_quad: int32 [32, 16, 24], P('tm', 'quad'), may hold values from 0 to 7
- block_tile: int32 [32, 16, 24], P('tm', 'quad'), may hold values from 0 to 1
- live_blocks: int32 [32, 16], P('tm', 'quad'), may hold values from 1 to 24, as said below
Outputs:
- mixed: bfloat16 [32, 2048, 192], P('tm', 'quad')
The draws below stay inside these ranges and needn't reach their ends.
Inputs may be any that keep to these rules, and one draw needn't show every extreme that they name: `live_blocks`: some device has every one of its query tiles at 24 live blocks; on a quarter of the devices or so all tiles are at 24.
All inputs are finite; a program needn't handle non-finite values.
Results may differ from the reference program's by a relative error of at most 0.008.
The reference program's roundings to bfloat16 on the way (of `probs` and `attended`) count: a program that leaves them out, or rounds other values in their place, can miss the bound.
Values may be sent and summed in bfloat16 or wider, within the bound.
No kernel may reach another device: no remote copies, remote signals or barrier semaphores. Data moves between devices by JAX's collectives and lax.ppermute only.
A program may use at most 64 MiB of HBM per device.

```python
import jax
import jax.numpy as jnp
from jax import lax

C = 192
HEADS = 6
TILE = 128
NB = 24
QT = 2
FRAMES = 32
CLIPS = 2
FRAME_TOK = 2048
FRAME_TILES = 16
N_QUAD = 8


def draw_features(key, part):
    base = jax.random.normal(key, (FRAMES, FRAME_TOK, C), jnp.float32)
    return jnp.clip(base, -6.0, 6.0).astype(jnp.bfloat16)


def draw_live_blocks(key, part):
    first, second, third = jax.random.split(key, 3)
    base = jax.random.randint(first, (FRAMES, FRAME_TILES), 1, NB + 1)
    device = jnp.arange(FRAMES, dtype=jnp.int32)[:, None] * N_QUAD + jnp.arange(FRAME_TILES, dtype=jnp.int32)[None, :] // QT
    busy = jax.random.randint(second, (FRAMES * N_QUAD,), 0, 4) == 0
    chosen = jax.random.randint(third, (), 0, FRAMES * N_QUAD)
    full = jnp.take(busy, device) | (device == chosen)
    return jnp.where(full, NB, base).astype(jnp.int32)


def place_ends(entries, stream_key, low, largest):
    place = [jax.random.randint(jax.random.fold_in(stream_key, axis), (), 0, length) for axis, length in enumerate(entries.shape)]
    widest = entries.shape.index(max(entries.shape))
    beside = place[:widest] + [(place[widest] + 1) % entries.shape[widest]] + place[widest + 1:]
    return entries.at[tuple(place)].set(low).at[tuple(beside)].set(largest)


def bell_draw(stream_key, extent, deviation, bound, kind=jnp.bfloat16):
    array = jax.random.normal(stream_key, extent, jnp.float32) * deviation
    return jnp.minimum(jnp.maximum(array, -bound), bound).astype(kind)


def setup_inputs(seed: int = 0) -> dict:
    key_list = jax.random.split(jax.random.key(seed), 10)
    features = draw_features(jax.random.fold_in(key_list[9], 71), 0)
    w_query = bell_draw(key_list[1], (C, C), (C // 9) ** -0.5, 1.25)
    w_key = bell_draw(key_list[2], (C, C), C ** -0.5, 0.4375)
    w_value = bell_draw(key_list[3], (C, C), C ** -0.5, 0.4375)
    w_out = bell_draw(key_list[4], (C, C), (C // 16) ** -0.5, 1.75)
    block_offset = place_ends(jax.random.randint(key_list[5], (FRAMES, FRAME_TILES, NB), 0, 3), jax.random.fold_in(key_list[5], 1), 0, 2).astype(jnp.int32)
    block_quad = place_ends(jax.random.randint(key_list[6], (FRAMES, FRAME_TILES, NB), 0, N_QUAD), jax.random.fold_in(key_list[6], 1), 0, N_QUAD - 1).astype(jnp.int32)
    block_tile = place_ends(jax.random.randint(key_list[7], (FRAMES, FRAME_TILES, NB), 0, QT), jax.random.fold_in(key_list[7], 1), 0, QT - 1).astype(jnp.int32)
    live_blocks = draw_live_blocks(jax.random.fold_in(key_list[9], 71), 0)
    return {"features": features, "w_query": w_query, "w_key": w_key, "w_value": w_value, "w_out": w_out, "block_offset": block_offset, "block_quad": block_quad, "block_tile": block_tile, "live_blocks": live_blocks}


def reference(features, w_query, w_key, w_value, w_out, block_offset, block_quad, block_tile, live_blocks):
    frames, frame_tok, width = features.shape
    head_dim = width // HEADS
    flat = features.reshape(frames * frame_tok, width)
    query = (jnp.dot(flat, w_query, preferred_element_type=jnp.float32) * (head_dim ** -0.5)).astype(jnp.bfloat16)
    keys = jnp.dot(flat, w_key, preferred_element_type=jnp.float32).astype(jnp.bfloat16)
    values = jnp.dot(flat, w_value, preferred_element_type=jnp.float32).astype(jnp.bfloat16)
    frame_tiles = frame_tok // TILE
    kv_tiles = jnp.stack([keys, values]).reshape(2, frames * frame_tiles, TILE * width)
    frame_ids = jnp.arange(frames, dtype=jnp.int32)
    before = (frame_ids - CLIPS) % frames
    after = (frame_ids + CLIPS) % frames
    own = frame_ids[:, None, None]
    source = jnp.where(block_offset == 0, before[:, None, None], jnp.where(block_offset == 1, own, after[:, None, None]))
    global_ids = (source * frame_tiles + block_quad * QT + block_tile).astype(jnp.int32)
    global_ids = global_ids.reshape(frames * frame_tiles, NB)
    counts = live_blocks.reshape(frames * frame_tiles)
    query_tiles = query.reshape(frames * frame_tiles, TILE, width)

    def attend(packed):
        qtile, ids, count = packed
        taken = jnp.take(kv_tiles, ids, axis=1).reshape(2, NB * TILE, HEADS, head_dim)
        qheads = qtile.reshape(TILE, HEADS, head_dim).astype(jnp.float32)
        scores = jnp.einsum('qhd,khd->hqk', qheads, taken[0].astype(jnp.float32))
        live = (jnp.arange(NB * TILE, dtype=jnp.int32) // TILE) < count
        scores = jnp.where(live[None, None, :], scores, -jnp.inf)
        top = jnp.max(scores, axis=-1, keepdims=True)
        weights = jnp.exp(scores - top)
        total = jnp.sum(weights, axis=-1)
        probs = weights.astype(jnp.bfloat16)
        summed = jnp.einsum('hqk,khd->qhd', probs.astype(jnp.float32), taken[1].astype(jnp.float32))
        return (summed / total.T[:, :, None]).astype(jnp.bfloat16).reshape(TILE, width)

    attended = lax.map(attend, (query_tiles, global_ids, counts))
    mixed = jnp.dot(attended.reshape(frames * frame_tok, width), w_out, preferred_element_type=jnp.float32)
    return mixed.astype(jnp.bfloat16).reshape(frames, frame_tok, width)
```

```python
import jax
import jax.numpy as jnp
from jax import lax
from jax.experimental import pallas as pl
from jax.experimental.pallas import tpu as pltpu
from jax.sharding import PartitionSpec as P

HEADS = 6
TILE = 128
NB = 24
LOOP = 16


def shifted(block, axis, distance):
    devices = range(lax.axis_size(axis))
    route = [((i - distance) % len(devices), i) for i in devices]
    return lax.ppermute(block, axis, route)


def attend_kernel(ids_ref, cnt_ref, q_ref, k_ref, v_ref, wo_ref, o_ref, kset, vset):
    i = pl.program_id(0)
    width = q_ref.shape[-1]
    head_dim = width // HEADS
    for b in range(NB):
        idx = ids_ref[i * NB + b]
        kset[pl.ds(b * TILE, TILE), :] = k_ref[idx]
        vset[pl.ds(b * TILE, TILE), :] = v_ref[idx]
    q = q_ref[0]
    count = cnt_ref[i]
    col = lax.broadcasted_iota(jnp.int32, (1, width), 1) // head_dim
    live = lax.broadcasted_iota(jnp.int32, (1, NB * TILE), 1) // TILE < count
    keys = kset[...]
    vals = vset[...]
    acc = jnp.zeros((TILE, width), jnp.float32)
    for h in range(HEADS):
        qm = jnp.where(col == h, q, jnp.zeros_like(q))
        scores = lax.dot_general(
            qm, keys, (((1,), (1,)), ((), ())), preferred_element_type=jnp.float32
        )
        scores = jnp.where(live, scores, -jnp.inf)
        top = jnp.max(scores, axis=1, keepdims=True)
        weights = jnp.exp(scores - top)
        total = jnp.sum(weights, axis=1, keepdims=True)
        probs = weights.astype(jnp.bfloat16)
        summed = jnp.dot(probs, vals, preferred_element_type=jnp.float32)
        acc = jnp.where(col == h, summed / total, acc)
    attended = acc.astype(jnp.bfloat16)
    o_ref[0] = jnp.dot(attended, wo_ref[...], preferred_element_type=jnp.float32).astype(
        o_ref.dtype
    )


def attend(ids, counts, query_tiles, key_tiles, value_tiles, w_out):
    n_q, _, width = query_tiles.shape
    n_kv = key_tiles.shape[0]
    full = lambda i, ids, cnt: (0, 0, 0)
    return pl.pallas_call(
        attend_kernel,
        out_shape=jax.ShapeDtypeStruct(query_tiles.shape, jnp.bfloat16),
        grid_spec=pltpu.PrefetchScalarGridSpec(
            num_scalar_prefetch=2,
            grid=(n_q,),
            in_specs=[
                pl.BlockSpec((1, TILE, width), lambda i, ids, cnt: (i, 0, 0)),
                pl.BlockSpec((n_kv, TILE, width), full),
                pl.BlockSpec((n_kv, TILE, width), full),
                pl.BlockSpec((width, width), lambda i, ids, cnt: (0, 0)),
            ],
            out_specs=pl.BlockSpec((1, TILE, width), lambda i, ids, cnt: (i, 0, 0)),
            scratch_shapes=[
                pltpu.VMEM((NB * TILE, width), jnp.bfloat16),
                pltpu.VMEM((NB * TILE, width), jnp.bfloat16),
            ],
        ),
        compiler_params=pltpu.CompilerParams(dimension_semantics=("arbitrary",)),
    )(ids, counts, query_tiles, key_tiles, value_tiles, w_out)


def body(
    features, w_query, w_key, w_value, w_out, block_offset, block_quad, block_tile, live_blocks
):
    tokens = features[0]
    tok_count, width = tokens.shape
    head_dim = width // HEADS
    tiles = tok_count // TILE
    pieces = lax.axis_size("quad")
    stride = lax.axis_size("tm") // LOOP
    query = (
        jnp.dot(tokens, w_query, preferred_element_type=jnp.float32) * head_dim ** (-0.5)
    ).astype(jnp.bfloat16)
    whole = lax.all_gather(tokens, "quad", axis=0, tiled=True)
    earlier = shifted(whole, "tm", stride)
    later = shifted(whole, "tm", -stride)
    window = jnp.concatenate([earlier, whole, later], axis=0)
    keys = jnp.dot(window, w_key, preferred_element_type=jnp.float32).astype(jnp.bfloat16)
    values = jnp.dot(window, w_value, preferred_element_type=jnp.float32).astype(jnp.bfloat16)
    n_kv = window.shape[0] // TILE
    key_tiles = keys.reshape(n_kv, TILE, width)
    value_tiles = values.reshape(n_kv, TILE, width)
    block_ids = block_offset[0] * (pieces * tiles) + block_quad[0] * tiles + block_tile[0]
    query_tiles = query.reshape(tiles, TILE, width)
    mixed = attend(
        block_ids.reshape(-1), live_blocks[0], query_tiles, key_tiles, value_tiles, w_out
    )
    return mixed.reshape(tok_count, width)[None]


def solution(mesh):
    return jax.shard_map(
        body,
        mesh=mesh,
        in_specs=(
            P("tm", "quad", None),
            P(),
            P(),
            P(),
            P(),
            P("tm", "quad", None),
            P("tm", "quad", None),
            P("tm", "quad", None),
            P("tm", "quad"),
        ),
        out_specs=P("tm", "quad", None),
        check_vma=False,
    )
```

```python
import jax
import jax.numpy as jnp
from jax import lax
from jax.experimental import pallas as pl
from jax.experimental.pallas import tpu as pltpu
from jax.sharding import PartitionSpec as P

HEADS = 6
TILE = 128
NB = 24
LOOP = 16


def attend_kernel(ids_ref, cnt_ref, qt_ref, kt_hbm, vt_hbm, wo_ref, o_ref, kset, vset, sems):
    i = pl.program_id(0)
    width = qt_ref.shape[0]
    head_dim = width // HEADS
    copies = []
    for b in range(NB):
        idx = ids_ref[i * NB + b]
        src = pl.ds(pl.multiple_of(idx * TILE, TILE), TILE)
        dst = pl.ds(b * TILE, TILE)
        ck = pltpu.make_async_copy(kt_hbm.at[:, src], kset.at[:, dst], sems.at[0, b])
        cv = pltpu.make_async_copy(vt_hbm.at[:, src], vset.at[:, dst], sems.at[1, b])
        ck.start()
        cv.start()
        copies.append((ck, cv))
    q = qt_ref[...].T
    count = cnt_ref[i]
    col = lax.broadcasted_iota(jnp.int32, (1, width), 1) // head_dim
    live = lax.broadcasted_iota(jnp.int32, (1, NB * TILE), 1) // TILE < count
    for ck, cv in copies:
        ck.wait()
        cv.wait()
    keys = kset[...]
    vals = vset[...]
    acc = jnp.zeros((TILE, width), jnp.float32)
    for h in range(HEADS):
        qm = jnp.where(col == h, q, jnp.zeros_like(q))
        scores = jnp.dot(qm, keys, preferred_element_type=jnp.float32)
        scores = jnp.where(live, scores, -jnp.inf)
        top = jnp.max(scores, axis=1, keepdims=True)
        weights = jnp.exp(scores - top)
        total = jnp.sum(weights, axis=1, keepdims=True)
        probs = weights.astype(jnp.bfloat16)
        summed = lax.dot_general(
            probs, vals, (((1,), (1,)), ((), ())), preferred_element_type=jnp.float32
        )
        acc = jnp.where(col == h, summed / total, acc)
    attended = acc.astype(jnp.bfloat16)
    mixed = jnp.dot(attended, wo_ref[...], preferred_element_type=jnp.float32)
    o_ref[...] = mixed.T.astype(o_ref.dtype)


def attend(ids, counts, query_t, key_t, value_t, w_out):
    width, n_tok = query_t.shape
    n_q = n_tok // TILE
    return pl.pallas_call(
        attend_kernel,
        out_shape=jax.ShapeDtypeStruct(query_t.shape, jnp.bfloat16),
        grid_spec=pltpu.PrefetchScalarGridSpec(
            num_scalar_prefetch=2,
            grid=(n_q,),
            in_specs=[
                pl.BlockSpec((width, TILE), lambda i, ids, cnt: (0, i)),
                pl.BlockSpec(memory_space=pl.ANY),
                pl.BlockSpec(memory_space=pl.ANY),
                pl.BlockSpec((width, width), lambda i, ids, cnt: (0, 0)),
            ],
            out_specs=pl.BlockSpec((width, TILE), lambda i, ids, cnt: (0, i)),
            scratch_shapes=[
                pltpu.VMEM((width, NB * TILE), jnp.bfloat16),
                pltpu.VMEM((width, NB * TILE), jnp.bfloat16),
                pltpu.SemaphoreType.DMA((2, NB)),
            ],
        ),
        compiler_params=pltpu.CompilerParams(dimension_semantics=("arbitrary",)),
    )(ids, counts, query_t, key_t, value_t, w_out)


def body(
    features, w_query, w_key, w_value, w_out, block_offset, block_quad, block_tile, live_blocks
):
    tokens_t = features[0].T
    width, tok_count = tokens_t.shape
    head_dim = width // HEADS
    tiles = tok_count // TILE
    n_tm = lax.axis_size("tm")
    n_quad = lax.axis_size("quad")
    stride = n_tm // LOOP
    query_t = (
        jnp.dot(w_query.T, tokens_t, preferred_element_type=jnp.float32) * head_dim ** (-0.5)
    ).astype(jnp.bfloat16)

    pieces = []
    for frame_step in (-1, 0, 1):
        for dq in range(n_quad):
            if frame_step == 0 and dq == 0:
                pieces.append(tokens_t)
                continue
            pairs = []
            for f in range(n_tm):
                for q in range(n_quad):
                    src = ((f + frame_step * stride) % n_tm) * n_quad + (q + dq) % n_quad
                    pairs.append((src, f * n_quad + q))
            pieces.append(lax.ppermute(tokens_t, ("tm", "quad"), pairs))
    window_t = jnp.concatenate(pieces, axis=1)
    key_t = jnp.dot(w_key.T, window_t, preferred_element_type=jnp.float32).astype(jnp.bfloat16)
    value_t = jnp.dot(w_value.T, window_t, preferred_element_type=jnp.float32).astype(
        jnp.bfloat16
    )
    my_quad = lax.axis_index("quad")
    rel_quad = (block_quad[0] - my_quad) % n_quad
    block_ids = block_offset[0] * (n_quad * tiles) + rel_quad * tiles + block_tile[0]
    mixed_t = attend(block_ids.reshape(-1), live_blocks[0], query_t, key_t, value_t, w_out)
    return mixed_t.T[None]


def solution(mesh):
    return jax.shard_map(
        body,
        mesh=mesh,
        in_specs=(
            P("tm", "quad", None),
            P(),
            P(),
            P(),
            P(),
            P("tm", "quad", None),
            P("tm", "quad", None),
            P("tm", "quad", None),
            P("tm", "quad"),
        ),
        out_specs=P("tm", "quad", None),
        check_vma=False,
    )
```

```python
import jax
import jax.numpy as jnp
from jax import lax
from jax.experimental import pallas as pl
from jax.experimental.pallas import tpu as pltpu
from jax.sharding import PartitionSpec as P

HEADS = 6
TILE = 128
NB = 24
LOOP = 16


def shifted(block, axis, distance):
    devices = range(lax.axis_size(axis))
    route = [((i - distance) % len(devices), i) for i in devices]
    return lax.ppermute(block, axis, route)


def attend_kernel(
    pos_ref, off_ref, cnt_ref, qt_ref, k0, k1, k2, v0, v1, v2, wo_ref, o_ref, kset, vset, sems
):
    i = pl.program_id(0)
    width = qt_ref.shape[0]
    head_dim = width // HEADS
    frames_k = (k0, k1, k2)
    frames_v = (v0, v1, v2)
    copies = []
    for b in range(NB):
        pos = pos_ref[i * NB + b]
        off = off_ref[i * NB + b]
        src = pl.ds(pl.multiple_of(pos * TILE, TILE), TILE)
        dst = pl.ds(b * TILE, TILE)
        for o in range(3):

            @pl.when(off == o)
            def _():
                pltpu.make_async_copy(frames_k[o].at[:, src], kset.at[:, dst], sems.at[0, b]).start()
                pltpu.make_async_copy(frames_v[o].at[:, src], vset.at[:, dst], sems.at[1, b]).start()

        copies.append(pltpu.make_async_copy(k0.at[:, src], kset.at[:, dst], sems.at[0, b]))
        copies.append(pltpu.make_async_copy(v0.at[:, src], vset.at[:, dst], sems.at[1, b]))
    q = qt_ref[...].T
    count = cnt_ref[i]
    col = lax.broadcasted_iota(jnp.int32, (1, width), 1) // head_dim
    live = lax.broadcasted_iota(jnp.int32, (1, NB * TILE), 1) // TILE < count
    for cp in copies:
        cp.wait()
    keys = kset[...]
    vals = vset[...]
    acc = jnp.zeros((TILE, width), jnp.float32)
    for h in range(HEADS):
        qm = jnp.where(col == h, q, jnp.zeros_like(q))
        scores = jnp.dot(qm, keys, preferred_element_type=jnp.float32)
        scores = jnp.where(live, scores, -jnp.inf)
        top = jnp.max(scores, axis=1, keepdims=True)
        weights = jnp.exp(scores - top)
        total = jnp.sum(weights, axis=1, keepdims=True)
        probs = weights.astype(jnp.bfloat16)
        summed = lax.dot_general(
            probs, vals, (((1,), (1,)), ((), ())), preferred_element_type=jnp.float32
        )
        acc = jnp.where(col == h, summed / total, acc)
    attended = acc.astype(jnp.bfloat16)
    mixed = jnp.dot(attended, wo_ref[...], preferred_element_type=jnp.float32)
    o_ref[...] = mixed.T.astype(o_ref.dtype)


def attend(pos, off, counts, query_t, keys_t, values_t, w_out):
    width, n_tok = query_t.shape
    n_q = n_tok // TILE
    hbm = pl.BlockSpec(memory_space=pl.ANY)
    return pl.pallas_call(
        attend_kernel,
        out_shape=jax.ShapeDtypeStruct(query_t.shape, jnp.bfloat16),
        grid_spec=pltpu.PrefetchScalarGridSpec(
            num_scalar_prefetch=3,
            grid=(n_q,),
            in_specs=[pl.BlockSpec((width, TILE), lambda i, *_: (0, i))]
            + [hbm] * 6
            + [pl.BlockSpec((width, width), lambda i, *_: (0, 0))],
            out_specs=pl.BlockSpec((width, TILE), lambda i, *_: (0, i)),
            scratch_shapes=[
                pltpu.VMEM((width, NB * TILE), jnp.bfloat16),
                pltpu.VMEM((width, NB * TILE), jnp.bfloat16),
                pltpu.SemaphoreType.DMA((2, NB)),
            ],
        ),
        compiler_params=pltpu.CompilerParams(dimension_semantics=("arbitrary",)),
    )(pos, off, counts, query_t, *keys_t, *values_t, w_out)


def project(w, x_t):
    return jnp.dot(w.T, x_t, preferred_element_type=jnp.float32).astype(jnp.bfloat16)


def body(
    features, w_query, w_key, w_value, w_out, block_offset, block_quad, block_tile, live_blocks
):
    tokens_t = features[0].T
    width, tok_count = tokens_t.shape
    head_dim = width // HEADS
    tiles = tok_count // TILE
    n_tm = lax.axis_size("tm")
    n_quad = lax.axis_size("quad")
    stride = n_tm // LOOP
    query_t = (
        jnp.dot(w_query.T, tokens_t, preferred_element_type=jnp.float32) * head_dim ** (-0.5)
    ).astype(jnp.bfloat16)
    pos = (block_quad[0] * tiles + block_tile[0]).reshape(-1)
    off = block_offset[0].reshape(-1)

    spread = jnp.tile(tokens_t, (1, n_quad))
    frame_t = lax.all_to_all(spread, "quad", 1, 1, tiled=True)
    earlier_t = shifted(frame_t, "tm", stride)
    later_t = shifted(frame_t, "tm", -stride)
    frames = (earlier_t, frame_t, later_t)
    keys_t = tuple(project(w_key, x) for x in frames)
    values_t = tuple(project(w_value, x) for x in frames)
    mixed_t = attend(pos, off, live_blocks[0], query_t, keys_t, values_t, w_out)
    return mixed_t.T[None]


def solution(mesh):
    return jax.shard_map(
        body,
        mesh=mesh,
        in_specs=(
            P("tm", "quad", None),
            P(),
            P(),
            P(),
            P(),
            P("tm", "quad", None),
            P("tm", "quad", None),
            P("tm", "quad", None),
            P("tm", "quad"),
        ),
        out_specs=P("tm", "quad", None),
        check_vma=False,
    )
```

```python
import jax
import jax.numpy as jnp
from jax import lax
from jax.experimental import pallas as pl
from jax.experimental.pallas import tpu as pltpu
from jax.sharding import PartitionSpec as P

HEADS = 6
TILE = 128
NB = 24
LOOP = 16


def shifted(block, axis, distance):
    devices = range(lax.axis_size(axis))
    route = [((i - distance) % len(devices), i) for i in devices]
    return lax.ppermute(block, axis, route)


def attend_kernel(
    pos_ref, off_ref, cnt_ref, qt_ref, k0, k1, k2, v0, v1, v2, wo_ref, o_ref, kset, vset, sems
):
    width, n_tok = qt_ref.shape
    n_q = n_tok // TILE
    head_dim = width // HEADS
    frames_k = (k0, k1, k2)
    frames_v = (v0, v1, v2)
    copies = []
    for t in range(n_q):
        waits = []
        for b in range(NB):
            pos = pos_ref[t * NB + b]
            off = off_ref[t * NB + b]
            src = pl.ds(pl.multiple_of(pos * TILE, TILE), TILE)
            dst = pl.ds(b * TILE, TILE)
            for o in range(3):

                @pl.when(off == o)
                def _():
                    pltpu.make_async_copy(
                        frames_k[o].at[:, src], kset.at[t, :, dst], sems.at[t, 0, b]
                    ).start()
                    pltpu.make_async_copy(
                        frames_v[o].at[:, src], vset.at[t, :, dst], sems.at[t, 1, b]
                    ).start()

            waits.append(pltpu.make_async_copy(k0.at[:, src], kset.at[t, :, dst], sems.at[t, 0, b]))
            waits.append(pltpu.make_async_copy(v0.at[:, src], vset.at[t, :, dst], sems.at[t, 1, b]))
        copies.append(waits)
    row = lax.broadcasted_iota(jnp.int32, (width, 1), 0) // head_dim
    key_block = lax.broadcasted_iota(jnp.int32, (NB * TILE, 1), 0) // TILE
    wo_t = wo_ref[...].T
    for t in range(n_q):
        q_t = qt_ref[:, pl.ds(t * TILE, TILE)]
        live = key_block < cnt_ref[t]
        for cp in copies[t]:
            cp.wait()
        keys = kset[t].T
        vals = vset[t]
        acc = jnp.zeros((width, TILE), jnp.float32)
        for h in range(HEADS):
            qm = jnp.where(row == h, q_t, jnp.zeros_like(q_t))
            scores = jnp.dot(keys, qm, preferred_element_type=jnp.float32)
            scores = jnp.where(live, scores, -jnp.inf)
            top = jnp.max(scores, axis=0, keepdims=True)
            weights = jnp.exp(scores - top)
            total = jnp.sum(weights, axis=0, keepdims=True)
            probs = weights.astype(jnp.bfloat16)
            summed = jnp.dot(vals, probs, preferred_element_type=jnp.float32)
            acc = jnp.where(row == h, summed / total, acc)
        attended = acc.astype(jnp.bfloat16)
        mixed = jnp.dot(wo_t, attended, preferred_element_type=jnp.float32)
        o_ref[:, pl.ds(t * TILE, TILE)] = mixed.astype(o_ref.dtype)


def attend(pos, off, counts, query_t, keys_t, values_t, w_out):
    width, n_tok = query_t.shape
    n_q = n_tok // TILE
    hbm = pl.BlockSpec(memory_space=pl.ANY)
    return pl.pallas_call(
        attend_kernel,
        out_shape=jax.ShapeDtypeStruct(query_t.shape, jnp.bfloat16),
        grid_spec=pltpu.PrefetchScalarGridSpec(
            num_scalar_prefetch=3,
            grid=(1,),
            in_specs=[pl.BlockSpec((width, n_tok), lambda i, *_: (0, 0))]
            + [hbm] * 6
            + [pl.BlockSpec((width, width), lambda i, *_: (0, 0))],
            out_specs=pl.BlockSpec((width, n_tok), lambda i, *_: (0, 0)),
            scratch_shapes=[
                pltpu.VMEM((n_q, width, NB * TILE), jnp.bfloat16),
                pltpu.VMEM((n_q, width, NB * TILE), jnp.bfloat16),
                pltpu.SemaphoreType.DMA((n_q, 2, NB)),
            ],
        ),
        compiler_params=pltpu.CompilerParams(dimension_semantics=("arbitrary",)),
    )(pos, off, counts, query_t, *keys_t, *values_t, w_out)


def project(w, x_t):
    return jnp.dot(w.T, x_t, preferred_element_type=jnp.float32).astype(jnp.bfloat16)


def body(
    features, w_query, w_key, w_value, w_out, block_offset, block_quad, block_tile, live_blocks
):
    tokens_t = features[0].T
    width, tok_count = tokens_t.shape
    head_dim = width // HEADS
    tiles = tok_count // TILE
    n_tm = lax.axis_size("tm")
    n_quad = lax.axis_size("quad")
    stride = n_tm // LOOP
    query_t = (
        jnp.dot(w_query.T, tokens_t, preferred_element_type=jnp.float32) * head_dim ** (-0.5)
    ).astype(jnp.bfloat16)
    rows = n_quad // 2
    my_quad = lax.axis_index("quad")
    my_row = my_quad // 2
    slot = ((block_quad[0] // 2 - my_row) % rows) * 2 + block_quad[0] % 2
    pos = (slot * tiles + block_tile[0]).reshape(-1)
    off = block_offset[0].reshape(-1)

    partner = lax.ppermute(tokens_t, "quad", [(q ^ 1, q) for q in range(n_quad)])
    pair = jnp.where(
        my_quad % 2 == 0,
        jnp.concatenate([tokens_t, partner], axis=1),
        jnp.concatenate([partner, tokens_t], axis=1),
    )
    rings = [pair]
    for d in range(1, rows):
        route = [((q + 2 * d) % n_quad, q) for q in range(n_quad)]
        rings.append(lax.ppermute(pair, "quad", route))
    frame_t = jnp.concatenate(rings, axis=1)
    earlier_t = shifted(frame_t, "tm", stride)
    later_t = shifted(frame_t, "tm", -stride)
    frames = (earlier_t, frame_t, later_t)
    keys_t = tuple(project(w_key, x) for x in frames)
    values_t = tuple(project(w_value, x) for x in frames)
    mixed_t = attend(pos, off, live_blocks[0], query_t, keys_t, values_t, w_out)
    return mixed_t.T[None]


def solution(mesh):
    return jax.shard_map(
        body,
        mesh=mesh,
        in_specs=(
            P("tm", "quad", None),
            P(),
            P(),
            P(),
            P(),
            P("tm", "quad", None),
            P("tm", "quad", None),
            P("tm", "quad", None),
            P("tm", "quad"),
        ),
        out_specs=P("tm", "quad", None),
        check_vma=False,
    )
```

```python
import jax
import jax.numpy as jnp
from jax import lax
from jax.experimental import pallas as pl
from jax.experimental.pallas import tpu as pltpu
from jax.sharding import PartitionSpec as P

HEADS = 6
TILE = 128
NB = 24
LOOP = 16


def shifted(block, axis, distance):
    devices = range(lax.axis_size(axis))
    route = [((i - distance) % len(devices), i) for i in devices]
    return lax.ppermute(block, axis, route)


def attend_kernel(
    pos_ref, off_ref, cnt_ref, qt_ref, k0, k1, k2, v0, v1, v2, wo_ref, o_ref, kset, vset, sems
):
    width, n_tok = qt_ref.shape
    n_q = n_tok // TILE
    head_dim = width // HEADS
    frames_k = (k0, k1, k2)
    frames_v = (v0, v1, v2)
    copies = []
    for t in range(n_q):
        waits = []
        for b in range(NB):
            pos = pos_ref[t * NB + b]
            off = off_ref[t * NB + b]
            src = pl.ds(pl.multiple_of(pos * TILE, TILE), TILE)
            dst = pl.ds(b * TILE, TILE)
            for o in range(3):

                @pl.when(off == o)
                def _():
                    pltpu.make_async_copy(
                        frames_k[o].at[:, src], kset.at[t, :, dst], sems.at[t, 0, b]
                    ).start()
                    pltpu.make_async_copy(
                        frames_v[o].at[:, src], vset.at[t, :, dst], sems.at[t, 1, b]
                    ).start()

            waits.append(pltpu.make_async_copy(k0.at[:, src], kset.at[t, :, dst], sems.at[t, 0, b]))
            waits.append(pltpu.make_async_copy(v0.at[:, src], vset.at[t, :, dst], sems.at[t, 1, b]))
        copies.append(waits)
    col = lax.broadcasted_iota(jnp.int32, (1, width), 1) // head_dim
    live_block = lax.broadcasted_iota(jnp.int32, (1, NB * TILE), 1) // TILE
    for t in range(n_q):
        q = qt_ref[:, pl.ds(t * TILE, TILE)].T
        live = live_block < cnt_ref[t]
        for cp in copies[t]:
            cp.wait()
        keys = kset[t]
        vals = vset[t]
        acc = jnp.zeros((TILE, width), jnp.float32)
        for h0 in range(0, HEADS, 2):
            qm = jnp.concatenate(
                [jnp.where(col == h, q, jnp.zeros_like(q)) for h in range(h0, h0 + 2)], axis=0
            )
            scores = jnp.dot(qm, keys, preferred_element_type=jnp.float32)
            scores = jnp.where(live, scores, -jnp.inf)
            top = jnp.max(scores, axis=1, keepdims=True)
            weights = jnp.exp(scores - top)
            total = jnp.sum(weights, axis=1, keepdims=True)
            probs = weights.astype(jnp.bfloat16)
            summed = lax.dot_general(
                probs, vals, (((1,), (1,)), ((), ())), preferred_element_type=jnp.float32
            )
            for j in range(2):
                part = summed[j * TILE:(j + 1) * TILE] / total[j * TILE:(j + 1) * TILE]
                acc = jnp.where(col == h0 + j, part, acc)
        attended = acc.astype(jnp.bfloat16)
        mixed = jnp.dot(attended, wo_ref[...], preferred_element_type=jnp.float32)
        o_ref[:, pl.ds(t * TILE, TILE)] = mixed.T.astype(o_ref.dtype)


def attend(pos, off, counts, query_t, keys_t, values_t, w_out):
    width, n_tok = query_t.shape
    n_q = n_tok // TILE
    hbm = pl.BlockSpec(memory_space=pl.ANY)
    return pl.pallas_call(
        attend_kernel,
        out_shape=jax.ShapeDtypeStruct(query_t.shape, jnp.bfloat16),
        grid_spec=pltpu.PrefetchScalarGridSpec(
            num_scalar_prefetch=3,
            grid=(1,),
            in_specs=[pl.BlockSpec((width, n_tok), lambda i, *_: (0, 0))]
            + [hbm] * 6
            + [pl.BlockSpec((width, width), lambda i, *_: (0, 0))],
            out_specs=pl.BlockSpec((width, n_tok), lambda i, *_: (0, 0)),
            scratch_shapes=[
                pltpu.VMEM((n_q, width, NB * TILE), jnp.bfloat16),
                pltpu.VMEM((n_q, width, NB * TILE), jnp.bfloat16),
                pltpu.SemaphoreType.DMA((n_q, 2, NB)),
            ],
        ),
        compiler_params=pltpu.CompilerParams(dimension_semantics=("arbitrary",), vmem_limit_bytes=48 * 1024 * 1024),
    )(pos, off, counts, query_t, *keys_t, *values_t, w_out)


def project(w, x_t):
    return jnp.dot(w.T, x_t, preferred_element_type=jnp.float32).astype(jnp.bfloat16)


def body(
    features, w_query, w_key, w_value, w_out, block_offset, block_quad, block_tile, live_blocks
):
    tokens_t = features[0].T
    width, tok_count = tokens_t.shape
    head_dim = width // HEADS
    tiles = tok_count // TILE
    n_tm = lax.axis_size("tm")
    n_quad = lax.axis_size("quad")
    stride = n_tm // LOOP
    query_t = (
        jnp.dot(w_query.T, tokens_t, preferred_element_type=jnp.float32) * head_dim ** (-0.5)
    ).astype(jnp.bfloat16)
    rows = n_quad // 2
    my_quad = lax.axis_index("quad")
    my_row = my_quad // 2
    slot = ((block_quad[0] // 2 - my_row) % rows) * 2 + block_quad[0] % 2
    pos = (slot * tiles + block_tile[0]).reshape(-1)
    off = block_offset[0].reshape(-1)

    partner = lax.ppermute(tokens_t, "quad", [(q ^ 1, q) for q in range(n_quad)])
    pair = jnp.where(
        my_quad % 2 == 0,
        jnp.concatenate([tokens_t, partner], axis=1),
        jnp.concatenate([partner, tokens_t], axis=1),
    )
    rings = [pair]
    for d in range(1, rows):
        route = [((q + 2 * d) % n_quad, q) for q in range(n_quad)]
        rings.append(lax.ppermute(pair, "quad", route))
    frame_t = jnp.concatenate(rings, axis=1)
    earlier_t = shifted(frame_t, "tm", stride)
    later_t = shifted(frame_t, "tm", -stride)
    frames = (earlier_t, frame_t, later_t)
    keys_t = tuple(project(w_key, x) for x in frames)
    values_t = tuple(project(w_value, x) for x in frames)
    mixed_t = attend(pos, off, live_blocks[0], query_t, keys_t, values_t, w_out)
    return mixed_t.T[None]


def solution(mesh):
    return jax.shard_map(
        body,
        mesh=mesh,
        in_specs=(
            P("tm", "quad", None),
            P(),
            P(),
            P(),
            P(),
            P("tm", "quad", None),
            P("tm", "quad", None),
            P("tm", "quad", None),
            P("tm", "quad"),
        ),
        out_specs=P("tm", "quad", None),
        check_vma=False,
    )
```

```python
import jax
import jax.numpy as jnp
from jax import lax
from jax.experimental import pallas as pl
from jax.experimental.pallas import tpu as pltpu
from jax.sharding import PartitionSpec as P

HEADS = 6
TILE = 128
NB = 24
LOOP = 16


def shifted(block, axis, distance):
    devices = range(lax.axis_size(axis))
    route = [((i - distance) % len(devices), i) for i in devices]
    return lax.ppermute(block, axis, route)


def attend_kernel(
    pos_ref, off_ref, cnt_ref, qt_ref, k0, k1, k2, v0, v1, v2, wo_ref, o_ref, kset, vset, sems
):
    width, n_tok = qt_ref.shape
    n_q = n_tok // TILE
    head_dim = width // HEADS
    frames_k = (k0, k1, k2)
    frames_v = (v0, v1, v2)
    copies = []
    for t in range(n_q):
        waits = []
        for b in range(NB):
            pos = pos_ref[t * NB + b]
            off = off_ref[t * NB + b]
            src = pl.ds(pl.multiple_of(pos * TILE, TILE), TILE)
            dst = pl.ds(b * TILE, TILE)
            for o in range(3):

                @pl.when(off == o)
                def _():
                    pltpu.make_async_copy(
                        frames_k[o].at[:, src], kset.at[t, :, dst], sems.at[t, 0, b]
                    ).start()
                    pltpu.make_async_copy(
                        frames_v[o].at[:, src], vset.at[t, :, dst], sems.at[t, 1, b]
                    ).start()

            waits.append(pltpu.make_async_copy(k0.at[:, src], kset.at[t, :, dst], sems.at[t, 0, b]))
            waits.append(pltpu.make_async_copy(v0.at[:, src], vset.at[t, :, dst], sems.at[t, 1, b]))
        copies.append(waits)
    col = lax.broadcasted_iota(jnp.int32, (1, width), 1) // head_dim
    live_block = lax.broadcasted_iota(jnp.int32, (1, NB * TILE), 1) // TILE
    for t in range(n_q):
        q = qt_ref[:, pl.ds(t * TILE, TILE)].T
        live = live_block < cnt_ref[t]
        for cp in copies[t]:
            cp.wait()
        keys = kset[t]
        vals = vset[t]
        acc = jnp.zeros((TILE, width), jnp.float32)
        for h0 in range(0, HEADS, 2):
            qm = jnp.concatenate(
                [jnp.where(col == h, q, jnp.zeros_like(q)) for h in range(h0, h0 + 2)], axis=0
            )
            scores = jnp.dot(qm, keys, preferred_element_type=jnp.float32)
            scores = jnp.where(live, scores, -jnp.inf)
            top = jnp.max(scores, axis=1, keepdims=True)
            weights = jnp.exp(scores - top)
            total = jnp.sum(weights, axis=1, keepdims=True)
            probs = weights.astype(jnp.bfloat16)
            summed = lax.dot_general(
                probs, vals, (((1,), (1,)), ((), ())), preferred_element_type=jnp.float32
            )
            for j in range(2):
                part = summed[j * TILE:(j + 1) * TILE] / total[j * TILE:(j + 1) * TILE]
                acc = jnp.where(col == h0 + j, part, acc)
        attended = acc.astype(jnp.bfloat16)
        mixed = jnp.dot(attended, wo_ref[...], preferred_element_type=jnp.float32)
        o_ref[:, pl.ds(t * TILE, TILE)] = mixed.T.astype(o_ref.dtype)


def attend(pos, off, counts, query_t, keys_t, values_t, w_out):
    width, n_tok = query_t.shape
    n_q = n_tok // TILE
    hbm = pl.BlockSpec(memory_space=pl.ANY)
    return pl.pallas_call(
        attend_kernel,
        out_shape=jax.ShapeDtypeStruct(query_t.shape, jnp.bfloat16),
        grid_spec=pltpu.PrefetchScalarGridSpec(
            num_scalar_prefetch=3,
            grid=(1,),
            in_specs=[pl.BlockSpec((width, n_tok), lambda i, *_: (0, 0))]
            + [hbm] * 6
            + [pl.BlockSpec((width, width), lambda i, *_: (0, 0))],
            out_specs=pl.BlockSpec((width, n_tok), lambda i, *_: (0, 0)),
            scratch_shapes=[
                pltpu.VMEM((n_q, width, NB * TILE), jnp.bfloat16),
                pltpu.VMEM((n_q, width, NB * TILE), jnp.bfloat16),
                pltpu.SemaphoreType.DMA((n_q, 2, NB)),
            ],
        ),
        compiler_params=pltpu.CompilerParams(dimension_semantics=("arbitrary",), vmem_limit_bytes=48 * 1024 * 1024),
    )(pos, off, counts, query_t, *keys_t, *values_t, w_out)


def project(w, x_t):
    return jnp.dot(w.T, x_t, preferred_element_type=jnp.float32).astype(jnp.bfloat16)


def body(
    features, w_query, w_key, w_value, w_out, block_offset, block_quad, block_tile, live_blocks
):
    tokens_t = features[0].T
    width, tok_count = tokens_t.shape
    head_dim = width // HEADS
    tiles = tok_count // TILE
    n_tm = lax.axis_size("tm")
    n_quad = lax.axis_size("quad")
    stride = n_tm // LOOP
    query_t = (
        jnp.dot(w_query.T, tokens_t, preferred_element_type=jnp.float32) * head_dim ** (-0.5)
    ).astype(jnp.bfloat16)
    rows = n_quad // 2
    my_quad = lax.axis_index("quad")
    my_row = my_quad // 2
    slot = ((block_quad[0] // 2 - my_row) % rows) * 2 + block_quad[0] % 2
    pos = (slot * tiles + block_tile[0]).reshape(-1)
    off = block_offset[0].reshape(-1)

    partner = lax.ppermute(tokens_t, "quad", [(q ^ 1, q) for q in range(n_quad)])
    pair = jnp.where(
        my_quad % 2 == 0,
        jnp.concatenate([tokens_t, partner], axis=1),
        jnp.concatenate([partner, tokens_t], axis=1),
    )
    rings = []
    for d in range(1, rows):
        route = [((q + 2 * d) % n_quad, q) for q in range(n_quad)]
        rings.append(lax.ppermute(pair, "quad", route))
    early_e = shifted(pair, "tm", stride)
    early_l = shifted(pair, "tm", -stride)
    rest = jnp.concatenate(rings, axis=1)
    frame_t = jnp.concatenate([pair, rest], axis=1)
    earlier_t = jnp.concatenate([early_e, shifted(rest, "tm", stride)], axis=1)
    later_t = jnp.concatenate([early_l, shifted(rest, "tm", -stride)], axis=1)
    frames = (earlier_t, frame_t, later_t)
    keys_t = tuple(project(w_key, x) for x in frames)
    values_t = tuple(project(w_value, x) for x in frames)
    mixed_t = attend(pos, off, live_blocks[0], query_t, keys_t, values_t, w_out)
    return mixed_t.T[None]


def solution(mesh):
    return jax.shard_map(
        body,
        mesh=mesh,
        in_specs=(
            P("tm", "quad", None),
            P(),
            P(),
            P(),
            P(),
            P("tm", "quad", None),
            P("tm", "quad", None),
            P("tm", "quad", None),
            P("tm", "quad"),
        ),
        out_specs=P("tm", "quad", None),
        check_vma=False,
    )
```

```python
import jax
import jax.numpy as jnp
from jax import lax
from jax.experimental import pallas as pl
from jax.experimental.pallas import tpu as pltpu
from jax.sharding import PartitionSpec as P

HEADS = 6
TILE = 128
NB = 24
LOOP = 16


def shifted(block, axis, distance):
    devices = range(lax.axis_size(axis))
    route = [((i - distance) % len(devices), i) for i in devices]
    return lax.ppermute(block, axis, route)


def attend_kernel(
    pos_ref, off_ref, cnt_ref, qt_ref, k0, k1, k2, v0, v1, v2, wo_ref, o_ref, kset, vset, sems
):
    width, n_tok = qt_ref.shape
    n_q = n_tok // TILE
    head_dim = width // HEADS
    frames_k = (k0, k1, k2)
    frames_v = (v0, v1, v2)
    copies = []
    for t in range(n_q):
        waits = []
        for b in range(NB):
            pos = pos_ref[t * NB + b]
            off = off_ref[t * NB + b]
            src = pl.ds(pl.multiple_of(pos * TILE, TILE), TILE)
            dst = pl.ds(b * TILE, TILE)
            for o in range(3):

                @pl.when(off == o)
                def _():
                    pltpu.make_async_copy(
                        frames_k[o].at[:, src], kset.at[t, :, dst], sems.at[t, 0, b]
                    ).start()
                    pltpu.make_async_copy(
                        frames_v[o].at[:, src], vset.at[t, :, dst], sems.at[t, 1, b]
                    ).start()

            waits.append(pltpu.make_async_copy(k0.at[:, src], kset.at[t, :, dst], sems.at[t, 0, b]))
            waits.append(pltpu.make_async_copy(v0.at[:, src], vset.at[t, :, dst], sems.at[t, 1, b]))
        copies.append(waits)
    col = lax.broadcasted_iota(jnp.int32, (1, width), 1) // head_dim
    live_block = lax.broadcasted_iota(jnp.int32, (1, NB * TILE), 1) // TILE
    for t in range(n_q):
        q = qt_ref[:, pl.ds(t * TILE, TILE)].T
        live = live_block < cnt_ref[t]
        for cp in copies[t]:
            cp.wait()
        keys = kset[t]
        vals = vset[t]
        acc = jnp.zeros((TILE, width), jnp.float32)
        for h0 in range(0, HEADS, 2):
            qm = jnp.concatenate(
                [jnp.where(col == h, q, jnp.zeros_like(q)) for h in range(h0, h0 + 2)], axis=0
            )
            scores = jnp.dot(qm, keys, preferred_element_type=jnp.float32)
            scores = jnp.where(live, scores, -jnp.inf)
            top = jnp.max(scores, axis=1, keepdims=True)
            weights = jnp.exp(scores - top)
            total = jnp.sum(weights, axis=1, keepdims=True)
            probs = weights.astype(jnp.bfloat16)
            summed = lax.dot_general(
                probs, vals, (((1,), (1,)), ((), ())), preferred_element_type=jnp.float32
            )
            for j in range(2):
                part = summed[j * TILE:(j + 1) * TILE] / total[j * TILE:(j + 1) * TILE]
                acc = jnp.where(col == h0 + j, part, acc)
        attended = acc.astype(jnp.bfloat16)
        mixed = jnp.dot(attended, wo_ref[...], preferred_element_type=jnp.float32)
        o_ref[:, pl.ds(t * TILE, TILE)] = mixed.T.astype(o_ref.dtype)


def attend(pos, off, counts, query_t, keys_t, values_t, w_out):
    width, n_tok = query_t.shape
    n_q = n_tok // TILE
    hbm = pl.BlockSpec(memory_space=pl.ANY)
    return pl.pallas_call(
        attend_kernel,
        out_shape=jax.ShapeDtypeStruct(query_t.shape, jnp.bfloat16),
        grid_spec=pltpu.PrefetchScalarGridSpec(
            num_scalar_prefetch=3,
            grid=(1,),
            in_specs=[pl.BlockSpec((width, n_tok), lambda i, *_: (0, 0))]
            + [hbm] * 6
            + [pl.BlockSpec((width, width), lambda i, *_: (0, 0))],
            out_specs=pl.BlockSpec((width, n_tok), lambda i, *_: (0, 0)),
            scratch_shapes=[
                pltpu.VMEM((n_q, width, NB * TILE), jnp.bfloat16),
                pltpu.VMEM((n_q, width, NB * TILE), jnp.bfloat16),
                pltpu.SemaphoreType.DMA((n_q, 2, NB)),
            ],
        ),
        compiler_params=pltpu.CompilerParams(dimension_semantics=("arbitrary",), vmem_limit_bytes=48 * 1024 * 1024),
    )(pos, off, counts, query_t, *keys_t, *values_t, w_out)


def project(w, x_t):
    return jnp.dot(w.T, x_t, preferred_element_type=jnp.float32).astype(jnp.bfloat16)


def body(
    features, w_query, w_key, w_value, w_out, block_offset, block_quad, block_tile, live_blocks
):
    tokens_t = features[0].T
    width, tok_count = tokens_t.shape
    head_dim = width // HEADS
    tiles = tok_count // TILE
    n_tm = lax.axis_size("tm")
    n_quad = lax.axis_size("quad")
    stride = n_tm // LOOP
    query_t = (
        jnp.dot(w_query.T, tokens_t, preferred_element_type=jnp.float32) * head_dim ** (-0.5)
    ).astype(jnp.bfloat16)
    rows = n_quad // 2
    my_quad = lax.axis_index("quad")
    my_row = my_quad // 2
    slot = ((block_quad[0] // 2 - my_row) % rows) * 2 + block_quad[0] % 2
    pos = (slot * tiles + block_tile[0]).reshape(-1)
    off = block_offset[0].reshape(-1)

    partner = lax.ppermute(tokens_t, "quad", [(q ^ 1, q) for q in range(n_quad)])
    pair = jnp.where(
        my_quad % 2 == 0,
        jnp.concatenate([tokens_t, partner], axis=1),
        jnp.concatenate([partner, tokens_t], axis=1),
    )
    rings = []
    for d in range(1, rows):
        route = [((q + 2 * d) % n_quad, q) for q in range(n_quad)]
        rings.append(lax.ppermute(pair, "quad", route))
    parts = [pair] + rings
    frame_t = jnp.concatenate(parts, axis=1)
    earlier_t = jnp.concatenate([shifted(x, "tm", stride) for x in parts], axis=1)
    later_t = jnp.concatenate([shifted(x, "tm", -stride) for x in parts], axis=1)
    frames = (earlier_t, frame_t, later_t)
    keys_t = tuple(project(w_key, x) for x in frames)
    values_t = tuple(project(w_value, x) for x in frames)
    mixed_t = attend(pos, off, live_blocks[0], query_t, keys_t, values_t, w_out)
    return mixed_t.T[None]


def solution(mesh):
    return jax.shard_map(
        body,
        mesh=mesh,
        in_specs=(
            P("tm", "quad", None),
            P(),
            P(),
            P(),
            P(),
            P("tm", "quad", None),
            P("tm", "quad", None),
            P("tm", "quad", None),
            P("tm", "quad"),
        ),
        out_specs=P("tm", "quad", None),
        check_vma=False,
    )
```

```python
import jax
import jax.numpy as jnp
from jax import lax
from jax.experimental import pallas as pl
from jax.experimental.pallas import tpu as pltpu
from jax.sharding import PartitionSpec as P

HEADS = 6
TILE = 128
NB = 24
LOOP = 16


def shifted(block, axis, distance):
    devices = range(lax.axis_size(axis))
    route = [((i - distance) % len(devices), i) for i in devices]
    return lax.ppermute(block, axis, route)


def attend_kernel(
    pos_ref, off_ref, cnt_ref, qt_ref, k0, k1, k2, v0, v1, v2, wo_ref, o_ref, kset, vset, sems
):
    width, n_tok = qt_ref.shape
    n_q = n_tok // TILE
    head_dim = width // HEADS
    frames_k = (k0, k1, k2)
    frames_v = (v0, v1, v2)
    copies = []
    for t in range(n_q):
        waits = []
        for b in range(NB):
            pos = pos_ref[t * NB + b]
            off = off_ref[t * NB + b]
            src = pl.ds(pl.multiple_of(pos * TILE, TILE), TILE)
            dst = pl.ds(b * TILE, TILE)
            for o in range(3):

                @pl.when(off == o)
                def _():
                    pltpu.make_async_copy(
                        frames_k[o].at[:, src], kset.at[t, :, dst], sems.at[t, 0, b]
                    ).start()
                    pltpu.make_async_copy(
                        frames_v[o].at[:, src], vset.at[t, :, dst], sems.at[t, 1, b]
                    ).start()

            waits.append(pltpu.make_async_copy(k0.at[:, src], kset.at[t, :, dst], sems.at[t, 0, b]))
            waits.append(pltpu.make_async_copy(v0.at[:, src], vset.at[t, :, dst], sems.at[t, 1, b]))
        copies.append(waits)
    col = lax.broadcasted_iota(jnp.int32, (1, width), 1) // head_dim
    live_block = lax.broadcasted_iota(jnp.int32, (1, NB * TILE), 1) // TILE
    for t in range(n_q):
        for cp in copies[t]:
            cp.wait()

        def tile_body(masked, t=t):
            live = live_block < cnt_ref[t]
            vals = vset[t]
            acc = jnp.zeros((TILE, width), jnp.float32)
            q_t = qt_ref[:, pl.ds(t * TILE, TILE)]
            for h0 in range(0, HEADS, 2):
                parts = []
                for h in (h0, h0 + 1):
                    q_h = q_t[h * head_dim:(h + 1) * head_dim, :].T
                    k_h = kset[t, h * head_dim:(h + 1) * head_dim, :]
                    parts.append(jnp.dot(q_h, k_h, preferred_element_type=jnp.float32))
                scores = jnp.concatenate(parts, axis=0)
                if masked:
                    scores = jnp.where(live, scores, -jnp.inf)
                top = jnp.max(scores, axis=1, keepdims=True)
                weights = jnp.exp(scores - top)
                total = jnp.sum(weights, axis=1, keepdims=True)
                probs = weights.astype(jnp.bfloat16)
                summed = lax.dot_general(
                    probs, vals, (((1,), (1,)), ((), ())), preferred_element_type=jnp.float32
                )
                for j in range(2):
                    part = summed[j * TILE:(j + 1) * TILE] / total[j * TILE:(j + 1) * TILE]
                    acc = jnp.where(col == h0 + j, part, acc)
            attended = acc.astype(jnp.bfloat16)
            mixed = jnp.dot(attended, wo_ref[...], preferred_element_type=jnp.float32)
            o_ref[:, pl.ds(t * TILE, TILE)] = mixed.T.astype(o_ref.dtype)

        full = cnt_ref[t] >= NB
        pl.when(full)(lambda: tile_body(False))
        pl.when(jnp.logical_not(full))(lambda: tile_body(True))


def attend(pos, off, counts, query_t, keys_t, values_t, w_out):
    width, n_tok = query_t.shape
    n_q = n_tok // TILE
    hbm = pl.BlockSpec(memory_space=pl.ANY)
    return pl.pallas_call(
        attend_kernel,
        out_shape=jax.ShapeDtypeStruct(query_t.shape, jnp.bfloat16),
        grid_spec=pltpu.PrefetchScalarGridSpec(
            num_scalar_prefetch=3,
            grid=(1,),
            in_specs=[pl.BlockSpec((width, n_tok), lambda i, *_: (0, 0))]
            + [hbm] * 6
            + [pl.BlockSpec((width, width), lambda i, *_: (0, 0))],
            out_specs=pl.BlockSpec((width, n_tok), lambda i, *_: (0, 0)),
            scratch_shapes=[
                pltpu.VMEM((n_q, width, NB * TILE), jnp.bfloat16),
                pltpu.VMEM((n_q, width, NB * TILE), jnp.bfloat16),
                pltpu.SemaphoreType.DMA((n_q, 2, NB)),
            ],
        ),
        compiler_params=pltpu.CompilerParams(dimension_semantics=("arbitrary",), vmem_limit_bytes=48 * 1024 * 1024),
    )(pos, off, counts, query_t, *keys_t, *values_t, w_out)


def project(w, x_t):
    return jnp.dot(w.T, x_t, preferred_element_type=jnp.float32).astype(jnp.bfloat16)


def body(
    features, w_query, w_key, w_value, w_out, block_offset, block_quad, block_tile, live_blocks
):
    tokens_t = features[0].T
    width, tok_count = tokens_t.shape
    head_dim = width // HEADS
    tiles = tok_count // TILE
    n_tm = lax.axis_size("tm")
    n_quad = lax.axis_size("quad")
    stride = n_tm // LOOP
    query_t = (
        jnp.dot(w_query.T, tokens_t, preferred_element_type=jnp.float32) * head_dim ** (-0.5)
    ).astype(jnp.bfloat16)
    rows = n_quad // 2
    my_quad = lax.axis_index("quad")
    my_row = my_quad // 2
    slot = ((block_quad[0] // 2 - my_row) % rows) * 2 + block_quad[0] % 2
    pos = (slot * tiles + block_tile[0]).reshape(-1)
    off = block_offset[0].reshape(-1)

    own_e = shifted(tokens_t, "tm", stride)
    own_l = shifted(tokens_t, "tm", -stride)
    partner = lax.ppermute(tokens_t, "quad", [(q ^ 1, q) for q in range(n_quad)])
    pair = jnp.where(
        my_quad % 2 == 0,
        jnp.concatenate([tokens_t, partner], axis=1),
        jnp.concatenate([partner, tokens_t], axis=1),
    )
    rings = []
    for d in range(1, rows):
        route = [((q + 2 * d) % n_quad, q) for q in range(n_quad)]
        rings.append(lax.ppermute(pair, "quad", route))
    rest = jnp.concatenate([partner] + rings, axis=1)
    frame_t = jnp.concatenate([pair] + rings, axis=1)
    rest_e = shifted(rest, "tm", stride)
    rest_l = shifted(rest, "tm", -stride)

    def assemble(own, moved):
        tail = moved[:, partner.shape[1]:]
        head = jnp.where(
            my_quad % 2 == 0,
            jnp.concatenate([own, moved[:, : partner.shape[1]]], axis=1),
            jnp.concatenate([moved[:, : partner.shape[1]], own], axis=1),
        )
        return jnp.concatenate([head, tail], axis=1)

    earlier_t = assemble(own_e, rest_e)
    later_t = assemble(own_l, rest_l)
    frames = (earlier_t, frame_t, later_t)
    keys_t = tuple(project(w_key, x) for x in frames)
    values_t = tuple(project(w_value, x) for x in frames)
    mixed_t = attend(pos, off, live_blocks[0], query_t, keys_t, values_t, w_out)
    return mixed_t.T[None]


def solution(mesh):
    return jax.shard_map(
        body,
        mesh=mesh,
        in_specs=(
            P("tm", "quad", None),
            P(),
            P(),
            P(),
            P(),
            P("tm", "quad", None),
            P("tm", "quad", None),
            P("tm", "quad", None),
            P("tm", "quad"),
        ),
        out_specs=P("tm", "quad", None),
        check_vma=False,
    )
```

```python
import jax
import jax.numpy as jnp
from jax import lax
from jax.experimental import pallas as pl
from jax.experimental.pallas import tpu as pltpu
from jax.sharding import PartitionSpec as P

HEADS = 6
TILE = 128
NB = 24
LOOP = 16


def shifted(block, axis, distance):
    devices = range(lax.axis_size(axis))
    route = [((i - distance) % len(devices), i) for i in devices]
    return lax.ppermute(block, axis, route)


def attend_kernel(
    pos_ref, off_ref, cnt_ref, qt_ref, k0, k1, k2, v0, v1, v2, wo_ref, o_ref, kset, vset, sems
):
    width, n_tok = qt_ref.shape
    n_q = n_tok // TILE
    head_dim = width // HEADS
    frames_k = (k0, k1, k2)
    frames_v = (v0, v1, v2)
    copies = []
    for t in range(n_q):
        waits = []
        for b in range(NB):
            pos = pos_ref[t * NB + b]
            off = off_ref[t * NB + b]
            src = pl.ds(pl.multiple_of(pos * TILE, TILE), TILE)
            dst = pl.ds(b * TILE, TILE)
            for o in range(3):

                @pl.when(off == o)
                def _():
                    pltpu.make_async_copy(
                        frames_k[o].at[:, src], kset.at[t, :, dst], sems.at[t, 0, b]
                    ).start()
                    pltpu.make_async_copy(
                        frames_v[o].at[:, src], vset.at[t, :, dst], sems.at[t, 1, b]
                    ).start()

            waits.append(pltpu.make_async_copy(k0.at[:, src], kset.at[t, :, dst], sems.at[t, 0, b]))
            waits.append(pltpu.make_async_copy(v0.at[:, src], vset.at[t, :, dst], sems.at[t, 1, b]))
        copies.append(waits)
    col = lax.broadcasted_iota(jnp.int32, (1, width), 1) // head_dim
    live_block = lax.broadcasted_iota(jnp.int32, (1, NB * TILE), 1) // TILE
    for t in range(n_q):
        q = qt_ref[:, pl.ds(t * TILE, TILE)].T
        live = live_block < cnt_ref[t]
        for cp in copies[t]:
            cp.wait()
        keys = kset[t]
        vals = vset[t]
        acc = jnp.zeros((TILE, width), jnp.float32)
        for h0 in range(0, HEADS, 2):
            qm = jnp.concatenate(
                [jnp.where(col == h, q, jnp.zeros_like(q)) for h in range(h0, h0 + 2)], axis=0
            )
            scores = jnp.dot(qm, keys, preferred_element_type=jnp.float32)
            scores = jnp.where(live, scores, -jnp.inf)
            top = jnp.max(scores, axis=1, keepdims=True)
            weights = jnp.exp(scores - top)
            total = jnp.sum(weights, axis=1, keepdims=True)
            probs = weights.astype(jnp.bfloat16)
            summed = lax.dot_general(
                probs, vals, (((1,), (1,)), ((), ())), preferred_element_type=jnp.float32
            )
            for j in range(2):
                part = summed[j * TILE:(j + 1) * TILE] / total[j * TILE:(j + 1) * TILE]
                acc = jnp.where(col == h0 + j, part, acc)
        attended = acc.astype(jnp.bfloat16)
        mixed = jnp.dot(attended, wo_ref[...], preferred_element_type=jnp.float32)
        o_ref[:, pl.ds(t * TILE, TILE)] = mixed.T.astype(o_ref.dtype)


def attend(pos, off, counts, query_t, keys_t, values_t, w_out):
    width, n_tok = query_t.shape
    n_q = n_tok // TILE
    hbm = pl.BlockSpec(memory_space=pl.ANY)
    return pl.pallas_call(
        attend_kernel,
        out_shape=jax.ShapeDtypeStruct(query_t.shape, jnp.bfloat16),
        grid_spec=pltpu.PrefetchScalarGridSpec(
            num_scalar_prefetch=3,
            grid=(1,),
            in_specs=[pl.BlockSpec((width, n_tok), lambda i, *_: (0, 0))]
            + [hbm] * 6
            + [pl.BlockSpec((width, width), lambda i, *_: (0, 0))],
            out_specs=pl.BlockSpec((width, n_tok), lambda i, *_: (0, 0)),
            scratch_shapes=[
                pltpu.VMEM((n_q, width, NB * TILE), jnp.bfloat16),
                pltpu.VMEM((n_q, width, NB * TILE), jnp.bfloat16),
                pltpu.SemaphoreType.DMA((n_q, 2, NB)),
            ],
        ),
        compiler_params=pltpu.CompilerParams(dimension_semantics=("arbitrary",), vmem_limit_bytes=48 * 1024 * 1024),
    )(pos, off, counts, query_t, *keys_t, *values_t, w_out)


def project(w, x_t):
    return jnp.dot(w.T, x_t, preferred_element_type=jnp.float32).astype(jnp.bfloat16)


def body(
    features, w_query, w_key, w_value, w_out, block_offset, block_quad, block_tile, live_blocks
):
    tokens_t = features[0].T
    width, tok_count = tokens_t.shape
    head_dim = width // HEADS
    tiles = tok_count // TILE
    n_tm = lax.axis_size("tm")
    n_quad = lax.axis_size("quad")
    stride = n_tm // LOOP
    query_t = (
        jnp.dot(w_query.T, tokens_t, preferred_element_type=jnp.float32) * head_dim ** (-0.5)
    ).astype(jnp.bfloat16)
    rows = n_quad // 2
    my_quad = lax.axis_index("quad")
    my_row = my_quad // 2
    slot = ((block_quad[0] // 2 - my_row) % rows) * 2 + block_quad[0] % 2
    pos = (slot * tiles + block_tile[0]).reshape(-1)
    off = block_offset[0].reshape(-1)

    partner = lax.ppermute(tokens_t, "quad", [(q ^ 1, q) for q in range(n_quad)])
    pair = jnp.where(
        my_quad % 2 == 0,
        jnp.concatenate([tokens_t, partner], axis=1),
        jnp.concatenate([partner, tokens_t], axis=1),
    )
    rings = []
    for d in range(1, rows):
        route = [((q + 2 * d) % n_quad, q) for q in range(n_quad)]
        rings.append(lax.ppermute(pair, "quad", route))
    early_e = shifted(pair, "tm", stride)
    early_l = shifted(pair, "tm", -stride)
    frame_t = jnp.concatenate([pair] + rings, axis=1)
    both = jnp.concatenate([early_e, early_l], axis=1)
    half = pair.shape[1]
    moved = []
    for d in range(1, rows):
        route = [((q + 2 * d) % n_quad, q) for q in range(n_quad)]
        moved.append(lax.ppermute(both, "quad", route))
    earlier_t = jnp.concatenate([early_e] + [m[:, :half] for m in moved], axis=1)
    later_t = jnp.concatenate([early_l] + [m[:, half:] for m in moved], axis=1)
    frames = (earlier_t, frame_t, later_t)
    keys_t = tuple(project(w_key, x) for x in frames)
    values_t = tuple(project(w_value, x) for x in frames)
    mixed_t = attend(pos, off, live_blocks[0], query_t, keys_t, values_t, w_out)
    return mixed_t.T[None]


def solution(mesh):
    return jax.shard_map(
        body,
        mesh=mesh,
        in_specs=(
            P("tm", "quad", None),
            P(),
            P(),
            P(),
            P(),
            P("tm", "quad", None),
            P("tm", "quad", None),
            P("tm", "quad", None),
            P("tm", "quad"),
        ),
        out_specs=P("tm", "quad", None),
        check_vma=False,
    )
```

```python
import jax
import jax.numpy as jnp
from jax import lax
from jax.experimental import pallas as pl
from jax.experimental.pallas import tpu as pltpu
from jax.sharding import PartitionSpec as P

HEADS = 6
TILE = 128
NB = 24
LOOP = 16


def shifted(block, axis, distance):
    devices = range(lax.axis_size(axis))
    route = [((i - distance) % len(devices), i) for i in devices]
    return lax.ppermute(block, axis, route)


def attend_kernel(
    pos_ref, off_ref, cnt_ref, qt_ref, k0, k1, k2, v0, v1, v2, wo_ref, o_ref, kset, vset, sems
):
    width, n_tok = qt_ref.shape
    n_q = n_tok // TILE
    head_dim = width // HEADS
    frames_k = (k0, k1, k2)
    frames_v = (v0, v1, v2)
    copies = []
    for t in range(n_q):
        waits = []
        for b in range(NB):
            pos = pos_ref[t * NB + b]
            off = off_ref[t * NB + b]
            src = pl.ds(pl.multiple_of(pos * TILE, TILE), TILE)
            dst = pl.ds(b * TILE, TILE)
            for o in range(3):

                @pl.when(off == o)
                def _():
                    pltpu.make_async_copy(
                        frames_k[o].at[:, src], kset.at[t, :, dst], sems.at[t, 0, b]
                    ).start()
                    pltpu.make_async_copy(
                        frames_v[o].at[:, src], vset.at[t, :, dst], sems.at[t, 1, b]
                    ).start()

            waits.append(pltpu.make_async_copy(k0.at[:, src], kset.at[t, :, dst], sems.at[t, 0, b]))
            waits.append(pltpu.make_async_copy(v0.at[:, src], vset.at[t, :, dst], sems.at[t, 1, b]))
        copies.append(waits)
    col = lax.broadcasted_iota(jnp.int32, (1, width), 1) // head_dim
    live_block = lax.broadcasted_iota(jnp.int32, (1, NB * TILE), 1) // TILE
    for t in range(n_q):
        q = qt_ref[:, pl.ds(t * TILE, TILE)].T
        live = live_block < cnt_ref[t]
        for cp in copies[t]:
            cp.wait()
        keys = kset[t]
        vals = vset[t]
        acc = jnp.zeros((TILE, width), jnp.float32)
        for h0 in range(0, HEADS, 2):
            qm = jnp.concatenate(
                [jnp.where(col == h, q, jnp.zeros_like(q)) for h in range(h0, h0 + 2)], axis=0
            )
            scores = jnp.dot(qm, keys, preferred_element_type=jnp.float32)
            scores = jnp.where(live, scores, -jnp.inf)
            top = jnp.max(scores, axis=1, keepdims=True)
            weights = jnp.exp(scores - top)
            total = jnp.sum(weights, axis=1, keepdims=True)
            probs = weights.astype(jnp.bfloat16)
            summed = lax.dot_general(
                probs, vals, (((1,), (1,)), ((), ())), preferred_element_type=jnp.float32
            )
            for j in range(2):
                part = summed[j * TILE:(j + 1) * TILE] / total[j * TILE:(j + 1) * TILE]
                acc = jnp.where(col == h0 + j, part, acc)
        attended = acc.astype(jnp.bfloat16)
        mixed = jnp.dot(attended, wo_ref[...], preferred_element_type=jnp.float32)
        o_ref[:, pl.ds(t * TILE, TILE)] = mixed.T.astype(o_ref.dtype)


def attend(pos, off, counts, query_t, keys_t, values_t, w_out):
    width, n_tok = query_t.shape
    n_q = n_tok // TILE
    hbm = pl.BlockSpec(memory_space=pl.ANY)
    return pl.pallas_call(
        attend_kernel,
        out_shape=jax.ShapeDtypeStruct(query_t.shape, jnp.bfloat16),
        grid_spec=pltpu.PrefetchScalarGridSpec(
            num_scalar_prefetch=3,
            grid=(1,),
            in_specs=[pl.BlockSpec((width, n_tok), lambda i, *_: (0, 0))]
            + [hbm] * 6
            + [pl.BlockSpec((width, width), lambda i, *_: (0, 0))],
            out_specs=pl.BlockSpec((width, n_tok), lambda i, *_: (0, 0)),
            scratch_shapes=[
                pltpu.VMEM((n_q, width, NB * TILE), jnp.bfloat16),
                pltpu.VMEM((n_q, width, NB * TILE), jnp.bfloat16),
                pltpu.SemaphoreType.DMA((n_q, 2, NB)),
            ],
        ),
        compiler_params=pltpu.CompilerParams(dimension_semantics=("arbitrary",), vmem_limit_bytes=48 * 1024 * 1024),
    )(pos, off, counts, query_t, *keys_t, *values_t, w_out)


def project(w, x_t):
    return jnp.dot(w.T, x_t, preferred_element_type=jnp.float32).astype(jnp.bfloat16)


def body(
    features, w_query, w_key, w_value, w_out, block_offset, block_quad, block_tile, live_blocks
):
    tokens_t = features[0].T
    width, tok_count = tokens_t.shape
    head_dim = width // HEADS
    tiles = tok_count // TILE
    n_tm = lax.axis_size("tm")
    n_quad = lax.axis_size("quad")
    stride = n_tm // LOOP
    query_t = (
        jnp.dot(w_query.T, tokens_t, preferred_element_type=jnp.float32) * head_dim ** (-0.5)
    ).astype(jnp.bfloat16)
    rows = n_quad // 2
    my_quad = lax.axis_index("quad")
    my_row = my_quad // 2
    slot = ((block_quad[0] // 2 - my_row) % rows) * 2 + block_quad[0] % 2
    pos = (slot * tiles + block_tile[0]).reshape(-1)
    off = block_offset[0].reshape(-1)

    partner = lax.ppermute(tokens_t, "quad", [(q ^ 1, q) for q in range(n_quad)])
    pair = jnp.where(
        my_quad % 2 == 0,
        jnp.concatenate([tokens_t, partner], axis=1),
        jnp.concatenate([partner, tokens_t], axis=1),
    )
    even = my_quad % 2 == 0
    rings = []
    for d in range(1, rows):
        route = [((q + 2 * d) % n_quad, q) for q in range(n_quad)]
        mine = lax.ppermute(tokens_t, "quad", route)
        theirs = lax.ppermute(partner, "quad", route)
        rings.append(
            jnp.where(
                even,
                jnp.concatenate([mine, theirs], axis=1),
                jnp.concatenate([theirs, mine], axis=1),
            )
        )
    early_e = shifted(pair, "tm", stride)
    early_l = shifted(pair, "tm", -stride)
    rest = jnp.concatenate(rings, axis=1)
    frame_t = jnp.concatenate([pair, rest], axis=1)
    earlier_t = jnp.concatenate([early_e, shifted(rest, "tm", stride)], axis=1)
    later_t = jnp.concatenate([early_l, shifted(rest, "tm", -stride)], axis=1)
    frames = (earlier_t, frame_t, later_t)
    keys_t = tuple(project(w_key, x) for x in frames)
    values_t = tuple(project(w_value, x) for x in frames)
    mixed_t = attend(pos, off, live_blocks[0], query_t, keys_t, values_t, w_out)
    return mixed_t.T[None]


def solution(mesh):
    return jax.shard_map(
        body,
        mesh=mesh,
        in_specs=(
            P("tm", "quad", None),
            P(),
            P(),
            P(),
            P(),
            P("tm", "quad", None),
            P("tm", "quad", None),
            P("tm", "quad", None),
            P("tm", "quad"),
        ),
        out_specs=P("tm", "quad", None),
        check_vma=False,
    )
```

```python
import jax
import jax.numpy as jnp
from jax import lax
from jax.experimental import pallas as pl
from jax.experimental.pallas import tpu as pltpu
from jax.sharding import PartitionSpec as P

HEADS = 6
TILE = 128
NB = 24
LOOP = 16


def shifted(block, axis, distance):
    devices = range(lax.axis_size(axis))
    route = [((i - distance) % len(devices), i) for i in devices]
    return lax.ppermute(block, axis, route)


def attend_kernel(
    pos_ref, off_ref, cnt_ref, qt_ref, k0, k1, k2, v0, v1, v2, wo_ref, o_ref, kset, vset, sems
):
    width, n_tok = qt_ref.shape
    n_q = n_tok // TILE
    head_dim = width // HEADS
    frames_k = (k0, k1, k2)
    frames_v = (v0, v1, v2)
    copies = []
    for t in range(n_q):
        waits = []
        for b in range(NB):
            pos = pos_ref[t * NB + b]
            off = off_ref[t * NB + b]
            src = pl.ds(pl.multiple_of(pos * TILE, TILE), TILE)
            dst = pl.ds(b * TILE, TILE)
            for o in range(3):

                @pl.when(off == o)
                def _():
                    pltpu.make_async_copy(
                        frames_k[o].at[:, src], kset.at[t, :, dst], sems.at[t, 0, b]
                    ).start()
                    pltpu.make_async_copy(
                        frames_v[o].at[:, src], vset.at[t, :, dst], sems.at[t, 1, b]
                    ).start()

            waits.append(pltpu.make_async_copy(k0.at[:, src], kset.at[t, :, dst], sems.at[t, 0, b]))
            waits.append(pltpu.make_async_copy(v0.at[:, src], vset.at[t, :, dst], sems.at[t, 1, b]))
        copies.append(waits)
    col = lax.broadcasted_iota(jnp.int32, (1, width), 1) // head_dim
    live_block = lax.broadcasted_iota(jnp.int32, (1, NB * TILE), 1) // TILE
    for t in range(n_q):
        q = qt_ref[:, pl.ds(t * TILE, TILE)].T
        live = live_block < cnt_ref[t]
        for cp in copies[t]:
            cp.wait()
        keys = kset[t]
        vals = vset[t]
        acc = jnp.zeros((TILE, width), jnp.float32)
        for h0 in range(0, HEADS, 2):
            qm = jnp.concatenate(
                [jnp.where(col == h, q, jnp.zeros_like(q)) for h in range(h0, h0 + 2)], axis=0
            )
            scores = jnp.dot(qm, keys, preferred_element_type=jnp.float32)
            scores = jnp.where(live, scores, -jnp.inf)
            top = jnp.max(scores, axis=1, keepdims=True)
            weights = jnp.exp(scores - top)
            total = jnp.sum(weights, axis=1, keepdims=True)
            probs = weights.astype(jnp.bfloat16)
            summed = lax.dot_general(
                probs, vals, (((1,), (1,)), ((), ())), preferred_element_type=jnp.float32
            )
            for j in range(2):
                part = summed[j * TILE:(j + 1) * TILE] / total[j * TILE:(j + 1) * TILE]
                acc = jnp.where(col == h0 + j, part, acc)
        attended = acc.astype(jnp.bfloat16)
        mixed = jnp.dot(attended, wo_ref[...], preferred_element_type=jnp.float32)
        o_ref[:, pl.ds(t * TILE, TILE)] = mixed.T.astype(o_ref.dtype)


def attend(pos, off, counts, query_t, keys_t, values_t, w_out):
    width, n_tok = query_t.shape
    n_q = n_tok // TILE
    hbm = pl.BlockSpec(memory_space=pl.ANY)
    return pl.pallas_call(
        attend_kernel,
        out_shape=jax.ShapeDtypeStruct(query_t.shape, jnp.bfloat16),
        grid_spec=pltpu.PrefetchScalarGridSpec(
            num_scalar_prefetch=3,
            grid=(1,),
            in_specs=[pl.BlockSpec((width, n_tok), lambda i, *_: (0, 0))]
            + [hbm] * 6
            + [pl.BlockSpec((width, width), lambda i, *_: (0, 0))],
            out_specs=pl.BlockSpec((width, n_tok), lambda i, *_: (0, 0)),
            scratch_shapes=[
                pltpu.VMEM((n_q, width, NB * TILE), jnp.bfloat16),
                pltpu.VMEM((n_q, width, NB * TILE), jnp.bfloat16),
                pltpu.SemaphoreType.DMA((n_q, 2, NB)),
            ],
        ),
        compiler_params=pltpu.CompilerParams(dimension_semantics=("arbitrary",), vmem_limit_bytes=48 * 1024 * 1024),
    )(pos, off, counts, query_t, *keys_t, *values_t, w_out)


def project(w, x_t):
    return jnp.dot(w.T, x_t, preferred_element_type=jnp.float32).astype(jnp.bfloat16)


def body(
    features, w_query, w_key, w_value, w_out, block_offset, block_quad, block_tile, live_blocks
):
    tokens_t = features[0].T
    width, tok_count = tokens_t.shape
    head_dim = width // HEADS
    tiles = tok_count // TILE
    n_tm = lax.axis_size("tm")
    n_quad = lax.axis_size("quad")
    stride = n_tm // LOOP
    query_t = (
        jnp.dot(w_query.T, tokens_t, preferred_element_type=jnp.float32) * head_dim ** (-0.5)
    ).astype(jnp.bfloat16)
    rows = n_quad // 2
    my_quad = lax.axis_index("quad")
    my_row = my_quad // 2
    slot = ((block_quad[0] // 2 - my_row) % rows) * 2 + block_quad[0] % 2
    pos = (slot * tiles + block_tile[0]).reshape(-1)
    off = block_offset[0].reshape(-1)

    partner = lax.ppermute(tokens_t, "quad", [(q ^ 1, q) for q in range(n_quad)])
    pair = jnp.where(
        my_quad % 2 == 0,
        jnp.concatenate([tokens_t, partner], axis=1),
        jnp.concatenate([partner, tokens_t], axis=1),
    )
    up = [((q + 2) % n_quad, q) for q in range(n_quad)]
    down = [((q - 2) % n_quad, q) for q in range(n_quad)]
    above = lax.ppermute(pair, "quad", up)
    below = lax.ppermute(pair, "quad", down)
    half = pair.shape[1] // 2
    across = jnp.concatenate(
        [
            lax.ppermute(above[:, :half], "quad", up),
            lax.ppermute(below[:, half:], "quad", down),
        ],
        axis=1,
    )
    rings = [above, across, below]
    early_e = shifted(pair, "tm", stride)
    early_l = shifted(pair, "tm", -stride)
    rest = jnp.concatenate(rings, axis=1)
    frame_t = jnp.concatenate([pair, rest], axis=1)
    earlier_t = jnp.concatenate([early_e, shifted(rest, "tm", stride)], axis=1)
    later_t = jnp.concatenate([early_l, shifted(rest, "tm", -stride)], axis=1)
    frames = (earlier_t, frame_t, later_t)
    keys_t = tuple(project(w_key, x) for x in frames)
    values_t = tuple(project(w_value, x) for x in frames)
    mixed_t = attend(pos, off, live_blocks[0], query_t, keys_t, values_t, w_out)
    return mixed_t.T[None]


def solution(mesh):
    return jax.shard_map(
        body,
        mesh=mesh,
        in_specs=(
            P("tm", "quad", None),
            P(),
            P(),
            P(),
            P(),
            P("tm", "quad", None),
            P("tm", "quad", None),
            P("tm", "quad", None),
            P("tm", "quad"),
        ),
        out_specs=P("tm", "quad", None),
        check_vma=False,
    )
```

```python
import jax
import jax.numpy as jnp
from jax import lax
from jax.experimental import pallas as pl
from jax.experimental.pallas import tpu as pltpu
from jax.sharding import PartitionSpec as P

HEADS = 6
TILE = 128
NB = 24
LOOP = 16


def shifted(block, axis, distance):
    devices = range(lax.axis_size(axis))
    route = [((i - distance) % len(devices), i) for i in devices]
    return lax.ppermute(block, axis, route)


def attend_kernel(
    pos_ref, off_ref, cnt_ref, qt_ref, k0, k1, k2, v0, v1, v2, wo_ref, o_ref, kset, vset, sems
):
    width, n_tok = qt_ref.shape
    n_q = n_tok // TILE
    head_dim = width // HEADS
    frames_k = (k0, k1, k2)
    frames_v = (v0, v1, v2)
    copies = []
    for t in range(n_q):
        waits = []
        for b in range(NB):
            pos = pos_ref[t * NB + b]
            off = off_ref[t * NB + b]
            src = pl.ds(pl.multiple_of(pos * TILE, TILE), TILE)
            dst = pl.ds(b * TILE, TILE)
            for o in range(3):

                @pl.when(off == o)
                def _():
                    pltpu.make_async_copy(
                        frames_k[o].at[:, src], kset.at[t, :, dst], sems.at[t, 0, b]
                    ).start()
                    pltpu.make_async_copy(
                        frames_v[o].at[:, src], vset.at[t, :, dst], sems.at[t, 1, b]
                    ).start()

            waits.append(pltpu.make_async_copy(k0.at[:, src], kset.at[t, :, dst], sems.at[t, 0, b]))
            waits.append(pltpu.make_async_copy(v0.at[:, src], vset.at[t, :, dst], sems.at[t, 1, b]))
        copies.append(waits)
    col = lax.broadcasted_iota(jnp.int32, (1, width), 1) // head_dim
    live_block = lax.broadcasted_iota(jnp.int32, (1, NB * TILE), 1) // TILE
    for t in range(n_q):
        q = qt_ref[:, pl.ds(t * TILE, TILE)].T
        live = live_block < cnt_ref[t]
        for cp in copies[t]:
            cp.wait()
        keys = kset[t]
        vals = vset[t]
        acc = jnp.zeros((TILE, width), jnp.float32)
        for h0 in range(0, HEADS, 2):
            qm = jnp.concatenate(
                [jnp.where(col == h, q, jnp.zeros_like(q)) for h in range(h0, h0 + 2)], axis=0
            )
            scores = jnp.dot(qm, keys, preferred_element_type=jnp.float32)
            scores = jnp.where(live, scores, -jnp.inf)
            top = jnp.max(scores, axis=1, keepdims=True)
            weights = jnp.exp(scores - top)
            total = jnp.sum(weights, axis=1, keepdims=True)
            probs = weights.astype(jnp.bfloat16)
            summed = lax.dot_general(
                probs, vals, (((1,), (1,)), ((), ())), preferred_element_type=jnp.float32
            )
            for j in range(2):
                part = summed[j * TILE:(j + 1) * TILE] / total[j * TILE:(j + 1) * TILE]
                acc = jnp.where(col == h0 + j, part, acc)
        attended = acc.astype(jnp.bfloat16)
        mixed = jnp.dot(attended, wo_ref[...], preferred_element_type=jnp.float32)
        o_ref[:, pl.ds(t * TILE, TILE)] = mixed.T.astype(o_ref.dtype)


def attend(pos, off, counts, query_t, keys_t, values_t, w_out):
    width, n_tok = query_t.shape
    n_q = n_tok // TILE
    hbm = pl.BlockSpec(memory_space=pl.ANY)
    return pl.pallas_call(
        attend_kernel,
        out_shape=jax.ShapeDtypeStruct(query_t.shape, jnp.bfloat16),
        grid_spec=pltpu.PrefetchScalarGridSpec(
            num_scalar_prefetch=3,
            grid=(1,),
            in_specs=[pl.BlockSpec((width, n_tok), lambda i, *_: (0, 0))]
            + [hbm] * 6
            + [pl.BlockSpec((width, width), lambda i, *_: (0, 0))],
            out_specs=pl.BlockSpec((width, n_tok), lambda i, *_: (0, 0)),
            scratch_shapes=[
                pltpu.VMEM((n_q, width, NB * TILE), jnp.bfloat16),
                pltpu.VMEM((n_q, width, NB * TILE), jnp.bfloat16),
                pltpu.SemaphoreType.DMA((n_q, 2, NB)),
            ],
        ),
        compiler_params=pltpu.CompilerParams(dimension_semantics=("arbitrary",), vmem_limit_bytes=48 * 1024 * 1024),
    )(pos, off, counts, query_t, *keys_t, *values_t, w_out)


def project(w, x_t):
    return jnp.dot(w.T, x_t, preferred_element_type=jnp.float32).astype(jnp.bfloat16)


def body(
    features, w_query, w_key, w_value, w_out, block_offset, block_quad, block_tile, live_blocks
):
    tokens_t = features[0].T
    width, tok_count = tokens_t.shape
    head_dim = width // HEADS
    tiles = tok_count // TILE
    n_tm = lax.axis_size("tm")
    n_quad = lax.axis_size("quad")
    stride = n_tm // LOOP
    query_t = (
        jnp.dot(w_query.T, tokens_t, preferred_element_type=jnp.float32) * head_dim ** (-0.5)
    ).astype(jnp.bfloat16)
    rows = n_quad // 2
    my_quad = lax.axis_index("quad")
    my_row = my_quad // 2
    slot = ((block_quad[0] // 2 - my_row) % rows) * 2 + block_quad[0] % 2
    pos = (slot * tiles + block_tile[0]).reshape(-1)
    off = block_offset[0].reshape(-1)

    partner = lax.ppermute(tokens_t, "quad", [(q ^ 1, q) for q in range(n_quad)])
    pair = jnp.where(
        my_quad % 2 == 0,
        jnp.concatenate([tokens_t, partner], axis=1),
        jnp.concatenate([partner, tokens_t], axis=1),
    )
    up = [((q + 2) % n_quad, q) for q in range(n_quad)]
    down = [((q - 2) % n_quad, q) for q in range(n_quad)]
    above = lax.ppermute(pair, "quad", up)
    below = lax.ppermute(pair, "quad", down)
    half = pair.shape[1] // 2
    across = jnp.concatenate(
        [
            lax.ppermute(above[:, :half], "quad", up),
            lax.ppermute(below[:, half:], "quad", down),
        ],
        axis=1,
    )
    near = jnp.concatenate([pair, above, below], axis=1)
    frame_t = jnp.concatenate([pair, above, across, below], axis=1)
    width2 = pair.shape[1]

    def neighbour(distance):
        moved = shifted(near, "tm", distance)
        far = shifted(across, "tm", distance)
        return jnp.concatenate([moved[:, : 2 * width2], far, moved[:, 2 * width2 :]], axis=1)

    earlier_t = neighbour(stride)
    later_t = neighbour(-stride)
    frames = (earlier_t, frame_t, later_t)
    keys_t = tuple(project(w_key, x) for x in frames)
    values_t = tuple(project(w_value, x) for x in frames)
    mixed_t = attend(pos, off, live_blocks[0], query_t, keys_t, values_t, w_out)
    return mixed_t.T[None]


def solution(mesh):
    return jax.shard_map(
        body,
        mesh=mesh,
        in_specs=(
            P("tm", "quad", None),
            P(),
            P(),
            P(),
            P(),
            P("tm", "quad", None),
            P("tm", "quad", None),
            P("tm", "quad", None),
            P("tm", "quad"),
        ),
        out_specs=P("tm", "quad", None),
        check_vma=False,
    )
```

```python
import jax
import jax.numpy as jnp
from jax import lax
from jax.experimental import pallas as pl
from jax.experimental.pallas import tpu as pltpu
from jax.sharding import PartitionSpec as P

HEADS = 6
TILE = 128
NB = 24
LOOP = 16


def shifted(block, axis, distance):
    devices = range(lax.axis_size(axis))
    route = [((i - distance) % len(devices), i) for i in devices]
    return lax.ppermute(block, axis, route)


def attend_kernel(pos_ref, off_ref, cnt_ref, qt_ref, *refs):
    n_src = (len(refs) - 5) // 2
    srcs_k = refs[:n_src]
    srcs_v = refs[n_src:2 * n_src]
    wo_ref, o_ref, kset, vset, sems = refs[2 * n_src:]
    k0 = srcs_k[0]
    v0 = srcs_v[0]
    width, n_tok = qt_ref.shape
    n_q = n_tok // TILE
    head_dim = width // HEADS
    copies = []
    for t in range(n_q):
        waits = []
        for b in range(NB):
            pos = pos_ref[t * NB + b]
            off = off_ref[t * NB + b]
            src = pl.ds(pl.multiple_of(pos * TILE, TILE), TILE)
            dst = pl.ds(b * TILE, TILE)
            for o in range(n_src):

                @pl.when(off == o)
                def _():
                    pltpu.make_async_copy(
                        srcs_k[o].at[:, src], kset.at[t, :, dst], sems.at[t, 0, b]
                    ).start()
                    pltpu.make_async_copy(
                        srcs_v[o].at[:, src], vset.at[t, :, dst], sems.at[t, 1, b]
                    ).start()

            waits.append(pltpu.make_async_copy(k0.at[:, src], kset.at[t, :, dst], sems.at[t, 0, b]))
            waits.append(pltpu.make_async_copy(v0.at[:, src], vset.at[t, :, dst], sems.at[t, 1, b]))
        copies.append(waits)
    col = lax.broadcasted_iota(jnp.int32, (1, width), 1) // head_dim
    live_block = lax.broadcasted_iota(jnp.int32, (1, NB * TILE), 1) // TILE
    for t in range(n_q):
        q = qt_ref[:, pl.ds(t * TILE, TILE)].T
        live = live_block < cnt_ref[t]
        for cp in copies[t]:
            cp.wait()
        keys = kset[t]
        vals = vset[t]
        acc = jnp.zeros((TILE, width), jnp.float32)
        for h0 in range(0, HEADS, 2):
            qm = jnp.concatenate(
                [jnp.where(col == h, q, jnp.zeros_like(q)) for h in range(h0, h0 + 2)], axis=0
            )
            scores = jnp.dot(qm, keys, preferred_element_type=jnp.float32)
            scores = jnp.where(live, scores, -jnp.inf)
            top = jnp.max(scores, axis=1, keepdims=True)
            weights = jnp.exp(scores - top)
            total = jnp.sum(weights, axis=1, keepdims=True)
            probs = weights.astype(jnp.bfloat16)
            summed = lax.dot_general(
                probs, vals, (((1,), (1,)), ((), ())), preferred_element_type=jnp.float32
            )
            for j in range(2):
                part = summed[j * TILE:(j + 1) * TILE] / total[j * TILE:(j + 1) * TILE]
                acc = jnp.where(col == h0 + j, part, acc)
        attended = acc.astype(jnp.bfloat16)
        mixed = jnp.dot(attended, wo_ref[...], preferred_element_type=jnp.float32)
        o_ref[:, pl.ds(t * TILE, TILE)] = mixed.T.astype(o_ref.dtype)


def attend(pos, off, counts, query_t, keys_t, values_t, w_out):
    width, n_tok = query_t.shape
    n_q = n_tok // TILE
    hbm = pl.BlockSpec(memory_space=pl.ANY)
    return pl.pallas_call(
        attend_kernel,
        out_shape=jax.ShapeDtypeStruct(query_t.shape, jnp.bfloat16),
        grid_spec=pltpu.PrefetchScalarGridSpec(
            num_scalar_prefetch=3,
            grid=(1,),
            in_specs=[pl.BlockSpec((width, n_tok), lambda i, *_: (0, 0))]
            + [hbm] * (len(keys_t) + len(values_t))
            + [pl.BlockSpec((width, width), lambda i, *_: (0, 0))],
            out_specs=pl.BlockSpec((width, n_tok), lambda i, *_: (0, 0)),
            scratch_shapes=[
                pltpu.VMEM((n_q, width, NB * TILE), jnp.bfloat16),
                pltpu.VMEM((n_q, width, NB * TILE), jnp.bfloat16),
                pltpu.SemaphoreType.DMA((n_q, 2, NB)),
            ],
        ),
        compiler_params=pltpu.CompilerParams(dimension_semantics=("arbitrary",), vmem_limit_bytes=48 * 1024 * 1024),
    )(pos, off, counts, query_t, *keys_t, *values_t, w_out)


def project(w, x_t):
    return jnp.dot(w.T, x_t, preferred_element_type=jnp.float32).astype(jnp.bfloat16)


def body(
    features, w_query, w_key, w_value, w_out, block_offset, block_quad, block_tile, live_blocks
):
    tokens_t = features[0].T
    width, tok_count = tokens_t.shape
    head_dim = width // HEADS
    tiles = tok_count // TILE
    n_tm = lax.axis_size("tm")
    n_quad = lax.axis_size("quad")
    stride = n_tm // LOOP
    query_t = (
        jnp.dot(w_query.T, tokens_t, preferred_element_type=jnp.float32) * head_dim ** (-0.5)
    ).astype(jnp.bfloat16)
    rows = n_quad // 2
    my_quad = lax.axis_index("quad")
    my_row = my_quad // 2
    slot = ((block_quad[0] // 2 - my_row) % rows) * 2 + block_quad[0] % 2
    pos = (slot * tiles + block_tile[0]).reshape(-1)
    off = block_offset[0].reshape(-1)

    partner = lax.ppermute(tokens_t, "quad", [(q ^ 1, q) for q in range(n_quad)])
    pair = jnp.where(
        my_quad % 2 == 0,
        jnp.concatenate([tokens_t, partner], axis=1),
        jnp.concatenate([partner, tokens_t], axis=1),
    )
    up = [((q + 2) % n_quad, q) for q in range(n_quad)]
    down = [((q - 2) % n_quad, q) for q in range(n_quad)]
    above = lax.ppermute(pair, "quad", up)
    below = lax.ppermute(pair, "quad", down)
    half = pair.shape[1] // 2
    across = jnp.concatenate(
        [
            lax.ppermute(above[:, :half], "quad", up),
            lax.ppermute(below[:, half:], "quad", down),
        ],
        axis=1,
    )
    near = jnp.concatenate([pair, above, below], axis=1)
    frame_t = jnp.concatenate([pair, above, across, below], axis=1)
    width2 = pair.shape[1]

    sources = (
        frame_t,
        shifted(near, "tm", stride),
        shifted(across, "tm", stride),
        shifted(near, "tm", -stride),
        shifted(across, "tm", -stride),
    )
    far_lo = 2 * width2 // TILE
    far_hi = 3 * width2 // TILE
    is_far = (pos >= far_lo) & (pos < far_hi)
    local = jnp.where(is_far, pos - far_lo, jnp.where(pos >= far_hi, pos - (far_hi - far_lo), pos))
    source_id = jnp.where(off == 1, 0, jnp.where(off == 0, 1, 3) + is_far.astype(off.dtype))
    local = jnp.where(off == 1, pos, local)
    keys_t = tuple(project(w_key, x) for x in sources)
    values_t = tuple(project(w_value, x) for x in sources)
    mixed_t = attend(local, source_id, live_blocks[0], query_t, keys_t, values_t, w_out)
    return mixed_t.T[None]


def solution(mesh):
    return jax.shard_map(
        body,
        mesh=mesh,
        in_specs=(
            P("tm", "quad", None),
            P(),
            P(),
            P(),
            P(),
            P("tm", "quad", None),
            P("tm", "quad", None),
            P("tm", "quad", None),
            P("tm", "quad"),
        ),
        out_specs=P("tm", "quad", None),
        check_vma=False,
    )
```

```python
import jax
import jax.numpy as jnp
from jax import lax
from jax.experimental import pallas as pl
from jax.experimental.pallas import tpu as pltpu
from jax.sharding import PartitionSpec as P

HEADS = 6
TILE = 128
NB = 24
LOOP = 16


def shifted(block, axis, distance):
    devices = range(lax.axis_size(axis))
    route = [((i - distance) % len(devices), i) for i in devices]
    return lax.ppermute(block, axis, route)


def attend_kernel(pos_ref, off_ref, cnt_ref, qt_ref, *refs):
    n_src = (len(refs) - 5) // 2
    srcs_k = refs[:n_src]
    srcs_v = refs[n_src:2 * n_src]
    wo_ref, o_ref, kset, vset, sems = refs[2 * n_src:]
    k0 = srcs_k[0]
    v0 = srcs_v[0]
    width, n_tok = qt_ref.shape
    n_q = n_tok // TILE
    head_dim = width // HEADS
    copies = []
    for t in range(n_q):
        waits = []
        for b in range(NB):
            pos = pos_ref[t * NB + b]
            off = off_ref[t * NB + b]
            src = pl.ds(pl.multiple_of(pos * TILE, TILE), TILE)
            dst = pl.ds(b * TILE, TILE)
            for o in range(n_src):

                @pl.when(off == o)
                def _():
                    pltpu.make_async_copy(
                        srcs_k[o].at[:, src], kset.at[t, :, dst], sems.at[t, 0, b]
                    ).start()
                    pltpu.make_async_copy(
                        srcs_v[o].at[:, src], vset.at[t, :, dst], sems.at[t, 1, b]
                    ).start()

            waits.append(pltpu.make_async_copy(k0.at[:, src], kset.at[t, :, dst], sems.at[t, 0, b]))
            waits.append(pltpu.make_async_copy(v0.at[:, src], vset.at[t, :, dst], sems.at[t, 1, b]))
        copies.append(waits)
    col = lax.broadcasted_iota(jnp.int32, (1, width), 1) // head_dim
    live_block = lax.broadcasted_iota(jnp.int32, (1, NB * TILE), 1) // TILE
    for t in range(n_q):
        q = qt_ref[:, pl.ds(t * TILE, TILE)].T
        live = live_block < cnt_ref[t]
        for cp in copies[t]:
            cp.wait()
        keys = kset[t]
        vals = vset[t]
        acc = jnp.zeros((TILE, width), jnp.float32)
        for h0 in range(0, HEADS, 2):
            qm = jnp.concatenate(
                [jnp.where(col == h, q, jnp.zeros_like(q)) for h in range(h0, h0 + 2)], axis=0
            )
            scores = jnp.dot(qm, keys, preferred_element_type=jnp.float32)
            scores = jnp.where(live, scores, -jnp.inf)
            top = jnp.max(scores, axis=1, keepdims=True)
            weights = jnp.exp(scores - top)
            total = jnp.sum(weights, axis=1, keepdims=True)
            probs = weights.astype(jnp.bfloat16)
            summed = lax.dot_general(
                probs, vals, (((1,), (1,)), ((), ())), preferred_element_type=jnp.float32
            )
            for j in range(2):
                part = summed[j * TILE:(j + 1) * TILE] / total[j * TILE:(j + 1) * TILE]
                acc = jnp.where(col == h0 + j, part, acc)
        attended = acc.astype(jnp.bfloat16)
        mixed = jnp.dot(attended, wo_ref[...], preferred_element_type=jnp.float32)
        o_ref[:, pl.ds(t * TILE, TILE)] = mixed.T.astype(o_ref.dtype)


def attend(pos, off, counts, query_t, keys_t, values_t, w_out):
    width, n_tok = query_t.shape
    n_q = n_tok // TILE
    hbm = pl.BlockSpec(memory_space=pl.ANY)
    return pl.pallas_call(
        attend_kernel,
        out_shape=jax.ShapeDtypeStruct(query_t.shape, jnp.bfloat16),
        grid_spec=pltpu.PrefetchScalarGridSpec(
            num_scalar_prefetch=3,
            grid=(1,),
            in_specs=[pl.BlockSpec((width, n_tok), lambda i, *_: (0, 0))]
            + [hbm] * (len(keys_t) + len(values_t))
            + [pl.BlockSpec((width, width), lambda i, *_: (0, 0))],
            out_specs=pl.BlockSpec((width, n_tok), lambda i, *_: (0, 0)),
            scratch_shapes=[
                pltpu.VMEM((n_q, width, NB * TILE), jnp.bfloat16),
                pltpu.VMEM((n_q, width, NB * TILE), jnp.bfloat16),
                pltpu.SemaphoreType.DMA((n_q, 2, NB)),
            ],
        ),
        compiler_params=pltpu.CompilerParams(dimension_semantics=("arbitrary",), vmem_limit_bytes=48 * 1024 * 1024),
    )(pos, off, counts, query_t, *keys_t, *values_t, w_out)


def project(w, x_t):
    return jnp.dot(w.T, x_t, preferred_element_type=jnp.float32).astype(jnp.bfloat16)


def body(
    features, w_query, w_key, w_value, w_out, block_offset, block_quad, block_tile, live_blocks
):
    tokens_t = features[0].T
    width, tok_count = tokens_t.shape
    head_dim = width // HEADS
    tiles = tok_count // TILE
    n_tm = lax.axis_size("tm")
    n_quad = lax.axis_size("quad")
    stride = n_tm // LOOP
    query_t = (
        jnp.dot(w_query.T, tokens_t, preferred_element_type=jnp.float32) * head_dim ** (-0.5)
    ).astype(jnp.bfloat16)
    rows = n_quad // 2
    my_quad = lax.axis_index("quad")
    my_row = my_quad // 2
    slot = ((block_quad[0] // 2 - my_row) % rows) * 2 + block_quad[0] % 2
    pos = (slot * tiles + block_tile[0]).reshape(-1)
    off = block_offset[0].reshape(-1)

    partner = lax.ppermute(tokens_t, "quad", [(q ^ 1, q) for q in range(n_quad)])
    pair = jnp.where(
        my_quad % 2 == 0,
        jnp.concatenate([tokens_t, partner], axis=1),
        jnp.concatenate([partner, tokens_t], axis=1),
    )
    up = [((q + 2) % n_quad, q) for q in range(n_quad)]
    down = [((q - 2) % n_quad, q) for q in range(n_quad)]
    above = lax.ppermute(pair, "quad", up)
    below = lax.ppermute(pair, "quad", down)
    half = pair.shape[1] // 2
    across = jnp.concatenate(
        [
            lax.ppermute(above[:, :half], "quad", up),
            lax.ppermute(below[:, half:], "quad", down),
        ],
        axis=1,
    )
    near = jnp.concatenate([pair, above, below], axis=1)
    frame_t = jnp.concatenate([pair, above, across, below], axis=1)
    width2 = pair.shape[1]

    sources = (
        frame_t,
        shifted(near, "tm", stride),
        shifted(across, "tm", stride),
        shifted(near, "tm", -stride),
        shifted(across, "tm", -stride),
    )
    far_lo = 2 * width2 // TILE
    far_hi = 3 * width2 // TILE
    is_far = (pos >= far_lo) & (pos < far_hi)
    local = jnp.where(is_far, pos - far_lo, jnp.where(pos >= far_hi, pos - (far_hi - far_lo), pos))
    source_id = jnp.where(off == 1, 0, jnp.where(off == 0, 1, 3) + is_far.astype(off.dtype))
    local = jnp.where(off == 1, pos, local)
    near_keys = [project(w_key, sources[i]) for i in (0, 1, 3)]
    near_values = [project(w_value, sources[i]) for i in (0, 1, 3)]
    far_e, far_l, near_keys, near_values = lax.optimization_barrier(
        (sources[2], sources[4], near_keys, near_values)
    )
    keys_t = (near_keys[0], near_keys[1], project(w_key, far_e), near_keys[2], project(w_key, far_l))
    values_t = (
        near_values[0],
        near_values[1],
        project(w_value, far_e),
        near_values[2],
        project(w_value, far_l),
    )
    mixed_t = attend(local, source_id, live_blocks[0], query_t, keys_t, values_t, w_out)
    return mixed_t.T[None]


def solution(mesh):
    return jax.shard_map(
        body,
        mesh=mesh,
        in_specs=(
            P("tm", "quad", None),
            P(),
            P(),
            P(),
            P(),
            P("tm", "quad", None),
            P("tm", "quad", None),
            P("tm", "quad", None),
            P("tm", "quad"),
        ),
        out_specs=P("tm", "quad", None),
        check_vma=False,
    )
```

```python
import jax
import jax.numpy as jnp
from jax import lax
from jax.experimental import pallas as pl
from jax.experimental.pallas import tpu as pltpu
from jax.sharding import PartitionSpec as P

HEADS = 6
TILE = 128
NB = 24
LOOP = 16


def shifted(block, axis, distance):
    devices = range(lax.axis_size(axis))
    route = [((i - distance) % len(devices), i) for i in devices]
    return lax.ppermute(block, axis, route)


def attend_kernel(pos_ref, off_ref, cnt_ref, qt_ref, *refs):
    n_src = (len(refs) - 5) // 2
    srcs_k = refs[:n_src]
    srcs_v = refs[n_src:2 * n_src]
    wo_ref, o_ref, kset, vset, sems = refs[2 * n_src:]
    k0 = srcs_k[0]
    v0 = srcs_v[0]
    width, n_tok = qt_ref.shape
    n_q = n_tok // TILE
    head_dim = width // HEADS
    copies = []
    for t in range(n_q):
        waits = []
        for b in range(NB):
            pos = pos_ref[t * NB + b]
            off = off_ref[t * NB + b]
            src = pl.ds(pl.multiple_of(pos * TILE, TILE), TILE)
            dst = pl.ds(b * TILE, TILE)
            for o in range(n_src):

                @pl.when(off == o)
                def _():
                    pltpu.make_async_copy(
                        srcs_k[o].at[:, src], kset.at[t, :, dst], sems.at[t, 0, b]
                    ).start()
                    pltpu.make_async_copy(
                        srcs_v[o].at[:, src], vset.at[t, :, dst], sems.at[t, 1, b]
                    ).start()

            waits.append(pltpu.make_async_copy(k0.at[:, src], kset.at[t, :, dst], sems.at[t, 0, b]))
            waits.append(pltpu.make_async_copy(v0.at[:, src], vset.at[t, :, dst], sems.at[t, 1, b]))
        copies.append(waits)
    col = lax.broadcasted_iota(jnp.int32, (1, width), 1) // head_dim
    live_block = lax.broadcasted_iota(jnp.int32, (1, NB * TILE), 1) // TILE
    for t in range(n_q):
        q = qt_ref[:, pl.ds(t * TILE, TILE)].T
        live = live_block < cnt_ref[t]
        for cp in copies[t]:
            cp.wait()
        keys = kset[t]
        vals = vset[t]
        acc = jnp.zeros((TILE, width), jnp.float32)
        for h0 in range(0, HEADS, 2):
            qm = jnp.concatenate(
                [jnp.where(col == h, q, jnp.zeros_like(q)) for h in range(h0, h0 + 2)], axis=0
            )
            scores = jnp.dot(qm, keys, preferred_element_type=jnp.float32)
            scores = jnp.where(live, scores, -jnp.inf)
            top = jnp.max(scores, axis=1, keepdims=True)
            weights = jnp.exp(scores - top)
            total = jnp.sum(weights, axis=1, keepdims=True)
            probs = weights.astype(jnp.bfloat16)
            summed = lax.dot_general(
                probs, vals, (((1,), (1,)), ((), ())), preferred_element_type=jnp.float32
            )
            for j in range(2):
                part = summed[j * TILE:(j + 1) * TILE] / total[j * TILE:(j + 1) * TILE]
                acc = jnp.where(col == h0 + j, part, acc)
        attended = acc.astype(jnp.bfloat16)
        mixed = jnp.dot(attended, wo_ref[...], preferred_element_type=jnp.float32)
        o_ref[:, pl.ds(t * TILE, TILE)] = mixed.T.astype(o_ref.dtype)


def attend(pos, off, counts, query_t, keys_t, values_t, w_out):
    width, n_tok = query_t.shape
    n_q = n_tok // TILE
    hbm = pl.BlockSpec(memory_space=pl.ANY)
    return pl.pallas_call(
        attend_kernel,
        out_shape=jax.ShapeDtypeStruct(query_t.shape, jnp.bfloat16),
        grid_spec=pltpu.PrefetchScalarGridSpec(
            num_scalar_prefetch=3,
            grid=(1,),
            in_specs=[pl.BlockSpec((width, n_tok), lambda i, *_: (0, 0))]
            + [hbm] * (len(keys_t) + len(values_t))
            + [pl.BlockSpec((width, width), lambda i, *_: (0, 0))],
            out_specs=pl.BlockSpec((width, n_tok), lambda i, *_: (0, 0)),
            scratch_shapes=[
                pltpu.VMEM((n_q, width, NB * TILE), jnp.bfloat16),
                pltpu.VMEM((n_q, width, NB * TILE), jnp.bfloat16),
                pltpu.SemaphoreType.DMA((n_q, 2, NB)),
            ],
        ),
        compiler_params=pltpu.CompilerParams(dimension_semantics=("arbitrary",), vmem_limit_bytes=48 * 1024 * 1024),
    )(pos, off, counts, query_t, *keys_t, *values_t, w_out)


def project(w, x_t):
    return jnp.dot(w.T, x_t, preferred_element_type=jnp.float32).astype(jnp.bfloat16)


def body(
    features, w_query, w_key, w_value, w_out, block_offset, block_quad, block_tile, live_blocks
):
    tokens_t = features[0].T
    width, tok_count = tokens_t.shape
    head_dim = width // HEADS
    tiles = tok_count // TILE
    n_tm = lax.axis_size("tm")
    n_quad = lax.axis_size("quad")
    stride = n_tm // LOOP
    query_t = (
        jnp.dot(w_query.T, tokens_t, preferred_element_type=jnp.float32) * head_dim ** (-0.5)
    ).astype(jnp.bfloat16)
    rows = n_quad // 2
    my_quad = lax.axis_index("quad")
    my_row = my_quad // 2
    slot = ((block_quad[0] // 2 - my_row) % rows) * 2 + block_quad[0] % 2
    pos = (slot * tiles + block_tile[0]).reshape(-1)
    off = block_offset[0].reshape(-1)

    partner = lax.ppermute(tokens_t, "quad", [(q ^ 1, q) for q in range(n_quad)])
    pair = jnp.where(
        my_quad % 2 == 0,
        jnp.concatenate([tokens_t, partner], axis=1),
        jnp.concatenate([partner, tokens_t], axis=1),
    )
    up = [((q + 2) % n_quad, q) for q in range(n_quad)]
    down = [((q - 2) % n_quad, q) for q in range(n_quad)]
    above = lax.ppermute(pair, "quad", up)
    below = lax.ppermute(pair, "quad", down)
    half = pair.shape[1] // 2
    across = jnp.concatenate(
        [
            lax.ppermute(above[:, :half], "quad", up),
            lax.ppermute(below[:, half:], "quad", down),
        ],
        axis=1,
    )
    near = jnp.concatenate([pair, above, below], axis=1)
    frame_t = jnp.concatenate([pair, above, across, below], axis=1)
    width2 = pair.shape[1]

    near_z, across_z = lax.optimization_barrier((near, across))
    sources = (
        frame_t,
        shifted(near_z, "tm", stride),
        shifted(across_z, "tm", stride),
        shifted(near_z, "tm", -stride),
        shifted(across_z, "tm", -stride),
    )
    far_lo = 2 * width2 // TILE
    far_hi = 3 * width2 // TILE
    is_far = (pos >= far_lo) & (pos < far_hi)
    local = jnp.where(is_far, pos - far_lo, jnp.where(pos >= far_hi, pos - (far_hi - far_lo), pos))
    source_id = jnp.where(off == 1, 0, jnp.where(off == 0, 1, 3) + is_far.astype(off.dtype))
    local = jnp.where(off == 1, pos, local)
    near_keys = [project(w_key, sources[i]) for i in (0, 1, 3)]
    near_values = [project(w_value, sources[i]) for i in (0, 1, 3)]
    far_e, far_l, near_keys, near_values = lax.optimization_barrier(
        (sources[2], sources[4], near_keys, near_values)
    )
    keys_t = (near_keys[0], near_keys[1], project(w_key, far_e), near_keys[2], project(w_key, far_l))
    values_t = (
        near_values[0],
        near_values[1],
        project(w_value, far_e),
        near_values[2],
        project(w_value, far_l),
    )
    mixed_t = attend(local, source_id, live_blocks[0], query_t, keys_t, values_t, w_out)
    return mixed_t.T[None]


def solution(mesh):
    return jax.shard_map(
        body,
        mesh=mesh,
        in_specs=(
            P("tm", "quad", None),
            P(),
            P(),
            P(),
            P(),
            P("tm", "quad", None),
            P("tm", "quad", None),
            P("tm", "quad", None),
            P("tm", "quad"),
        ),
        out_specs=P("tm", "quad", None),
        check_vma=False,
    )
```

```python
import jax
import jax.numpy as jnp
from jax import lax
from jax.experimental import pallas as pl
from jax.experimental.pallas import tpu as pltpu
from jax.sharding import PartitionSpec as P

HEADS = 6
TILE = 128
NB = 24
LOOP = 16


def shifted(block, axis, distance):
    devices = range(lax.axis_size(axis))
    route = [((i - distance) % len(devices), i) for i in devices]
    return lax.ppermute(block, axis, route)


def attend_kernel(pos_ref, off_ref, cnt_ref, qt_ref, *refs):
    n_src = (len(refs) - 5) // 2
    srcs_k = refs[:n_src]
    srcs_v = refs[n_src:2 * n_src]
    wo_ref, o_ref, kset, vset, sems = refs[2 * n_src:]
    k0 = srcs_k[0]
    v0 = srcs_v[0]
    width, n_tok = qt_ref.shape
    n_q = n_tok // TILE
    head_dim = width // HEADS
    copies = []
    for t in range(n_q):
        waits = []
        for b in range(NB):
            pos = pos_ref[t * NB + b]
            off = off_ref[t * NB + b]
            src = pl.ds(pl.multiple_of(pos * TILE, TILE), TILE)
            dst = pl.ds(b * TILE, TILE)
            for o in range(n_src):

                @pl.when(off == o)
                def _():
                    pltpu.make_async_copy(
                        srcs_k[o].at[:, src], kset.at[t, :, dst], sems.at[t, 0, b]
                    ).start()
                    pltpu.make_async_copy(
                        srcs_v[o].at[:, src], vset.at[t, :, dst], sems.at[t, 1, b]
                    ).start()

            waits.append(pltpu.make_async_copy(k0.at[:, src], kset.at[t, :, dst], sems.at[t, 0, b]))
            waits.append(pltpu.make_async_copy(v0.at[:, src], vset.at[t, :, dst], sems.at[t, 1, b]))
        copies.append(waits)
    col = lax.broadcasted_iota(jnp.int32, (1, width), 1) // head_dim
    live_block = lax.broadcasted_iota(jnp.int32, (1, NB * TILE), 1) // TILE
    for t in range(n_q):
        q = qt_ref[:, pl.ds(t * TILE, TILE)].T
        live = live_block < cnt_ref[t]
        for cp in copies[t]:
            cp.wait()
        keys = kset[t]
        vals = vset[t]
        acc = jnp.zeros((TILE, width), jnp.float32)
        for h0 in range(0, HEADS, 2):
            qm = jnp.concatenate(
                [jnp.where(col == h, q, jnp.zeros_like(q)) for h in range(h0, h0 + 2)], axis=0
            )
            scores = jnp.dot(qm, keys, preferred_element_type=jnp.float32)
            scores = jnp.where(live, scores, -jnp.inf)
            top = jnp.max(scores, axis=1, keepdims=True)
            weights = jnp.exp(scores - top)
            total = jnp.sum(weights, axis=1, keepdims=True)
            probs = weights.astype(jnp.bfloat16)
            summed = lax.dot_general(
                probs, vals, (((1,), (1,)), ((), ())), preferred_element_type=jnp.float32
            )
            for j in range(2):
                part = summed[j * TILE:(j + 1) * TILE] / total[j * TILE:(j + 1) * TILE]
                acc = jnp.where(col == h0 + j, part, acc)
        attended = acc.astype(jnp.bfloat16)
        mixed = jnp.dot(attended, wo_ref[...], preferred_element_type=jnp.float32)
        o_ref[:, pl.ds(t * TILE, TILE)] = mixed.T.astype(o_ref.dtype)


def attend(pos, off, counts, query_t, keys_t, values_t, w_out):
    width, n_tok = query_t.shape
    n_q = n_tok // TILE
    hbm = pl.BlockSpec(memory_space=pl.ANY)
    return pl.pallas_call(
        attend_kernel,
        out_shape=jax.ShapeDtypeStruct(query_t.shape, jnp.bfloat16),
        grid_spec=pltpu.PrefetchScalarGridSpec(
            num_scalar_prefetch=3,
            grid=(1,),
            in_specs=[pl.BlockSpec((width, n_tok), lambda i, *_: (0, 0))]
            + [hbm] * (len(keys_t) + len(values_t))
            + [pl.BlockSpec((width, width), lambda i, *_: (0, 0))],
            out_specs=pl.BlockSpec((width, n_tok), lambda i, *_: (0, 0)),
            scratch_shapes=[
                pltpu.VMEM((n_q, width, NB * TILE), jnp.bfloat16),
                pltpu.VMEM((n_q, width, NB * TILE), jnp.bfloat16),
                pltpu.SemaphoreType.DMA((n_q, 2, NB)),
            ],
        ),
        compiler_params=pltpu.CompilerParams(dimension_semantics=("arbitrary",), vmem_limit_bytes=48 * 1024 * 1024),
    )(pos, off, counts, query_t, *keys_t, *values_t, w_out)


def project(w, x_t):
    return jnp.dot(w.T, x_t, preferred_element_type=jnp.float32).astype(jnp.bfloat16)


def body(
    features, w_query, w_key, w_value, w_out, block_offset, block_quad, block_tile, live_blocks
):
    tokens_t = features[0].T
    width, tok_count = tokens_t.shape
    head_dim = width // HEADS
    tiles = tok_count // TILE
    n_tm = lax.axis_size("tm")
    n_quad = lax.axis_size("quad")
    stride = n_tm // LOOP
    query_t = (
        jnp.dot(w_query.T, tokens_t, preferred_element_type=jnp.float32) * head_dim ** (-0.5)
    ).astype(jnp.bfloat16)
    rows = n_quad // 2
    my_quad = lax.axis_index("quad")
    my_row = my_quad // 2
    slot = ((block_quad[0] // 2 - my_row) % rows) * 2 + block_quad[0] % 2
    pos = (slot * tiles + block_tile[0]).reshape(-1)
    off = block_offset[0].reshape(-1)

    partner = lax.ppermute(tokens_t, "quad", [(q ^ 1, q) for q in range(n_quad)])
    pair = jnp.where(
        my_quad % 2 == 0,
        jnp.concatenate([tokens_t, partner], axis=1),
        jnp.concatenate([partner, tokens_t], axis=1),
    )
    up = [((q + 2) % n_quad, q) for q in range(n_quad)]
    down = [((q - 2) % n_quad, q) for q in range(n_quad)]
    above = lax.ppermute(pair, "quad", up)
    below = lax.ppermute(pair, "quad", down)
    half = pair.shape[1] // 2
    across = jnp.concatenate(
        [
            lax.ppermute(above[:, :half], "quad", up),
            lax.ppermute(below[:, half:], "quad", down),
        ],
        axis=1,
    )
    near = jnp.concatenate([pair, above, below], axis=1)
    frame_t = jnp.concatenate([pair, above, across, below], axis=1)
    width2 = pair.shape[1]

    sources = (
        frame_t,
        shifted(near, "tm", stride),
        shifted(across, "tm", stride),
        shifted(near, "tm", -stride),
        shifted(across, "tm", -stride),
    )
    far_lo = 2 * width2 // TILE
    far_hi = 3 * width2 // TILE
    is_far = (pos >= far_lo) & (pos < far_hi)
    local = jnp.where(is_far, pos - far_lo, jnp.where(pos >= far_hi, pos - (far_hi - far_lo), pos))
    source_id = jnp.where(off == 1, 0, jnp.where(off == 0, 1, 3) + is_far.astype(off.dtype))
    local = jnp.where(off == 1, pos, local)
    local = jnp.where((off == 2) & is_far, local + (far_hi - far_lo), local)
    source_id = jnp.where(source_id == 4, 2, source_id)
    near_keys = [project(w_key, sources[i]) for i in (0, 1, 3)]
    near_values = [project(w_value, sources[i]) for i in (0, 1, 3)]
    far_e, far_l, near_keys, near_values = lax.optimization_barrier(
        (sources[2], sources[4], near_keys, near_values)
    )
    far_both = jnp.concatenate([far_e, far_l], axis=1)
    far_key = project(w_key, far_both)
    far_value = project(w_value, far_both)
    keys_t = (near_keys[0], near_keys[1], far_key, near_keys[2])
    values_t = (near_values[0], near_values[1], far_value, near_values[2])
    mixed_t = attend(local, source_id, live_blocks[0], query_t, keys_t, values_t, w_out)
    return mixed_t.T[None]


def solution(mesh):
    return jax.shard_map(
        body,
        mesh=mesh,
        in_specs=(
            P("tm", "quad", None),
            P(),
            P(),
            P(),
            P(),
            P("tm", "quad", None),
            P("tm", "quad", None),
            P("tm", "quad", None),
            P("tm", "quad"),
        ),
        out_specs=P("tm", "quad", None),
        check_vma=False,
    )
```

```python
import jax
import jax.numpy as jnp
from jax import lax
from jax.experimental import pallas as pl
from jax.experimental.pallas import tpu as pltpu
from jax.sharding import PartitionSpec as P

HEADS = 6
TILE = 128
NB = 24
LOOP = 16


def shifted(block, axis, distance):
    devices = range(lax.axis_size(axis))
    route = [((i - distance) % len(devices), i) for i in devices]
    return lax.ppermute(block, axis, route)


def attend_kernel(pos_ref, off_ref, cnt_ref, qt_ref, *refs):
    n_src = (len(refs) - 5) // 2
    srcs_k = refs[:n_src]
    srcs_v = refs[n_src:2 * n_src]
    wo_ref, o_ref, kset, vset, sems = refs[2 * n_src:]
    k0 = srcs_k[0]
    v0 = srcs_v[0]
    width, n_tok = qt_ref.shape
    n_q = n_tok // TILE
    head_dim = width // HEADS
    copies = []
    for t in range(n_q):
        waits = []
        for b in range(NB):
            pos = pos_ref[t * NB + b]
            off = off_ref[t * NB + b]
            src = pl.ds(pl.multiple_of(pos * TILE, TILE), TILE)
            dst = pl.ds(b * TILE, TILE)
            for o in range(n_src):

                @pl.when(off == o)
                def _():
                    pltpu.make_async_copy(
                        srcs_k[o].at[:, src], kset.at[t, :, dst], sems.at[t, 0, b]
                    ).start()
                    pltpu.make_async_copy(
                        srcs_v[o].at[:, src], vset.at[t, :, dst], sems.at[t, 1, b]
                    ).start()

            waits.append(pltpu.make_async_copy(k0.at[:, src], kset.at[t, :, dst], sems.at[t, 0, b]))
            waits.append(pltpu.make_async_copy(v0.at[:, src], vset.at[t, :, dst], sems.at[t, 1, b]))
        copies.append(waits)
    col = lax.broadcasted_iota(jnp.int32, (1, width), 1) // head_dim
    live_block = lax.broadcasted_iota(jnp.int32, (1, NB * TILE), 1) // TILE
    for t in range(n_q):
        for cp in copies[t]:
            cp.wait()

        def tile_body(masked, t=t):
            q = qt_ref[:, pl.ds(t * TILE, TILE)].T
            live = live_block < cnt_ref[t]
            keys = kset[t]
            vals = vset[t]
            acc = jnp.zeros((TILE, width), jnp.float32)
            for h0 in range(0, HEADS, 2):
                qm = jnp.concatenate(
                    [jnp.where(col == h, q, jnp.zeros_like(q)) for h in range(h0, h0 + 2)], axis=0
                )
                scores = jnp.dot(qm, keys, preferred_element_type=jnp.float32)
                if masked:
                    scores = jnp.where(live, scores, -jnp.inf)
                top = jnp.max(scores, axis=1, keepdims=True)
                weights = jnp.exp(scores - top)
                total = jnp.sum(weights, axis=1, keepdims=True)
                probs = weights.astype(jnp.bfloat16)
                summed = lax.dot_general(
                    probs, vals, (((1,), (1,)), ((), ())), preferred_element_type=jnp.float32
                )
                for j in range(2):
                    part = summed[j * TILE:(j + 1) * TILE] / total[j * TILE:(j + 1) * TILE]
                    acc = jnp.where(col == h0 + j, part, acc)
            attended = acc.astype(jnp.bfloat16)
            mixed = jnp.dot(attended, wo_ref[...], preferred_element_type=jnp.float32)
            o_ref[:, pl.ds(t * TILE, TILE)] = mixed.T.astype(o_ref.dtype)

        full = cnt_ref[t] >= NB
        pl.when(full)(lambda: tile_body(False))
        pl.when(jnp.logical_not(full))(lambda: tile_body(True))


def attend(pos, off, counts, query_t, keys_t, values_t, w_out):
    width, n_tok = query_t.shape
    n_q = n_tok // TILE
    hbm = pl.BlockSpec(memory_space=pl.ANY)
    return pl.pallas_call(
        attend_kernel,
        out_shape=jax.ShapeDtypeStruct(query_t.shape, jnp.bfloat16),
        grid_spec=pltpu.PrefetchScalarGridSpec(
            num_scalar_prefetch=3,
            grid=(1,),
            in_specs=[pl.BlockSpec((width, n_tok), lambda i, *_: (0, 0))]
            + [hbm] * (len(keys_t) + len(values_t))
            + [pl.BlockSpec((width, width), lambda i, *_: (0, 0))],
            out_specs=pl.BlockSpec((width, n_tok), lambda i, *_: (0, 0)),
            scratch_shapes=[
                pltpu.VMEM((n_q, width, NB * TILE), jnp.bfloat16),
                pltpu.VMEM((n_q, width, NB * TILE), jnp.bfloat16),
                pltpu.SemaphoreType.DMA((n_q, 2, NB)),
            ],
        ),
        compiler_params=pltpu.CompilerParams(dimension_semantics=("arbitrary",), vmem_limit_bytes=48 * 1024 * 1024),
    )(pos, off, counts, query_t, *keys_t, *values_t, w_out)


def project(w, x_t):
    return jnp.dot(w.T, x_t, preferred_element_type=jnp.float32).astype(jnp.bfloat16)


def body(
    features, w_query, w_key, w_value, w_out, block_offset, block_quad, block_tile, live_blocks
):
    tokens_t = features[0].T
    width, tok_count = tokens_t.shape
    head_dim = width // HEADS
    tiles = tok_count // TILE
    n_tm = lax.axis_size("tm")
    n_quad = lax.axis_size("quad")
    stride = n_tm // LOOP
    query_t = (
        jnp.dot(w_query.T, tokens_t, preferred_element_type=jnp.float32) * head_dim ** (-0.5)
    ).astype(jnp.bfloat16)
    rows = n_quad // 2
    my_quad = lax.axis_index("quad")
    my_row = my_quad // 2
    slot = ((block_quad[0] // 2 - my_row) % rows) * 2 + block_quad[0] % 2
    pos = (slot * tiles + block_tile[0]).reshape(-1)
    off = block_offset[0].reshape(-1)

    partner = lax.ppermute(tokens_t, "quad", [(q ^ 1, q) for q in range(n_quad)])
    pair = jnp.where(
        my_quad % 2 == 0,
        jnp.concatenate([tokens_t, partner], axis=1),
        jnp.concatenate([partner, tokens_t], axis=1),
    )
    up = [((q + 2) % n_quad, q) for q in range(n_quad)]
    down = [((q - 2) % n_quad, q) for q in range(n_quad)]
    above = lax.ppermute(pair, "quad", up)
    below = lax.ppermute(pair, "quad", down)
    half = pair.shape[1] // 2
    across = jnp.concatenate(
        [
            lax.ppermute(above[:, :half], "quad", up),
            lax.ppermute(below[:, half:], "quad", down),
        ],
        axis=1,
    )
    near = jnp.concatenate([pair, above, below], axis=1)
    frame_t = jnp.concatenate([pair, above, across, below], axis=1)
    width2 = pair.shape[1]

    sources = (
        frame_t,
        shifted(near, "tm", stride),
        shifted(across, "tm", stride),
        shifted(near, "tm", -stride),
        shifted(across, "tm", -stride),
    )
    far_lo = 2 * width2 // TILE
    far_hi = 3 * width2 // TILE
    is_far = (pos >= far_lo) & (pos < far_hi)
    local = jnp.where(is_far, pos - far_lo, jnp.where(pos >= far_hi, pos - (far_hi - far_lo), pos))
    source_id = jnp.where(off == 1, 0, jnp.where(off == 0, 1, 3) + is_far.astype(off.dtype))
    local = jnp.where(off == 1, pos, local)
    local = jnp.where((off == 2) & is_far, local + (far_hi - far_lo), local)
    source_id = jnp.where(source_id == 4, 2, source_id)
    near_keys = [project(w_key, sources[i]) for i in (0, 1, 3)]
    near_values = [project(w_value, sources[i]) for i in (0, 1, 3)]
    far_e, far_l, near_keys, near_values = lax.optimization_barrier(
        (sources[2], sources[4], near_keys, near_values)
    )
    far_both = jnp.concatenate([far_e, far_l], axis=1)
    far_key = project(w_key, far_both)
    far_value = project(w_value, far_both)
    keys_t = (near_keys[0], near_keys[1], far_key, near_keys[2])
    values_t = (near_values[0], near_values[1], far_value, near_values[2])
    mixed_t = attend(local, source_id, live_blocks[0], query_t, keys_t, values_t, w_out)
    return mixed_t.T[None]


def solution(mesh):
    return jax.shard_map(
        body,
        mesh=mesh,
        in_specs=(
            P("tm", "quad", None),
            P(),
            P(),
            P(),
            P(),
            P("tm", "quad", None),
            P("tm", "quad", None),
            P("tm", "quad", None),
            P("tm", "quad"),
        ),
        out_specs=P("tm", "quad", None),
        check_vma=False,
    )
```
